256 devices in a mesh: gx: 8 (over z), gy: 4 (over x_lo, core), gz: 8 (over y, x_hi).
Axes of the slice: x: 4 (x_hi: 2, x_lo: 2; x = x_hi * 2 + x_lo), y: 4, z: 8, core: 2. Of those that a mesh axis runs over, the one named last changes fastest.
Arguments:
- displacement: float32 [3, 128, 32, 1024], P(None, 'gx', 'gy', 'gz'), may hold values from -3 to 3
- velocity: float32 [3, 128, 32, 1024], P(None, 'gx', 'gy', 'gz'), may hold values from -6 to 6
- bulk_modulus: float32 [128, 32, 1024], P('gx', 'gy', 'gz'), may hold values from 3000 to 20000
- shear_modulus: float32 [128, 32, 1024], P('gx', 'gy', 'gz'), may hold values from 300 to 1500
- blast_load: float32 [3, 128, 32, 1024], P(None, 'gx', 'gy', 'gz'), may hold values from -50 to 50
- loaded: int32 [128, 32, 1024], P('gx', 'gy', 'gz'), may hold values 0 or 1
- broken: int32 [16, 128, 32, 1024], P(None, 'gx', 'gy', 'gz'), may hold values from 0 to 255, as said below
Outputs:
- new_displacement: float32 [3, 128, 32, 1024], P(None, 'gx', 'gy', 'gz')
- new_velocity: float32 [3, 128, 32, 1024], P(None, 'gx', 'gy', 'gz')
The draws below stay inside these ranges and needn't reach their ends.
Inputs may be any that keep to these rules, and one draw needn't show every extreme that they name: Bit j of word w, that is (broken // 2^j) % 2, is the broken flag of offset 8 w + j in the reference program' numbering; bits of offsets 122 to 127 are zero. A bond's flag is the same at both of its ends: the flag of offset k at node i equals that of offset k + 61 at node i + o_k whenever that node lies in the lattice, for k under 61.
All inputs are finite; a program needn't handle non-finite values. No bound on the sum of `loaded` on one device may be relied on, other than what follows from the above.
Results may differ from the reference program's by a relative error of at most 0.0001.
Values sent between devices are 32-bit elements; how exact they have to be, the bound alone decides.
No kernel may reach another device: no remote copies, remote signals or barrier semaphores. Data moves between devices by JAX's collectives and lax.ppermute only.
A program may use at most 128 MiB of HBM per device.

```python
import math
import jax
import jax.numpy as jnp
import numpy as np
from jax import lax

STEPS = 2
NX = 128
NY = 32
NZ = 1024


def offset_table_drawn():
    forward = []
    for step_x in range(-3, 4):
        for step_y in range(-3, 4):
            for step_z in range(-3, 4):
                squared = step_x * step_x + step_y * step_y + step_z * step_z
                if squared == 0 or squared > 9:
                    continue
                summed = step_x + step_y + step_z
                if summed > 0 or (summed == 0 and (step_x > 0 or (step_x == 0 and step_y > 0))):
                    forward.append((step_x, step_y, step_z))
    return forward


def draw_broken(key, part):
    forward = offset_table_drawn()
    packed_words = [jnp.zeros((NX, NY, NZ), jnp.int32) for position in range(16)]
    for number in range(61):
        broken_bits = (jax.random.randint(jax.random.fold_in(key, number), (NX, NY, NZ), 0, 4) == 0).astype(jnp.int32)
        entry = forward[number]
        mirrored = jnp.roll(broken_bits, (entry[0], entry[1], entry[2]), axis=(0, 1, 2))
        packed_words[number // 8] = packed_words[number // 8] + broken_bits * 2 ** (number % 8)
        packed_words[(number + 61) // 8] = packed_words[(number + 61) // 8] + mirrored * 2 ** ((number + 61) % 8)
    return jnp.stack(packed_words)


def place_ends(values, own_key, low, top_value):
    longest = values.shape.index(max(values.shape))
    spots = []
    for shift in (0, 1):
        where = [jax.random.randint(jax.random.fold_in(own_key, axis), (), 0, length) for axis, length in enumerate(values.shape)]
        where[longest] = (where[longest] + shift) % values.shape[longest]
        spots.append(tuple(where))
    return values.at[spots[0]].set(low).at[spots[1]].set(top_value)


def block_levels(own_key, extent, pieces, smallest, high):
    def one(dim, blocks):
        draws = jax.random.uniform(jax.random.fold_in(jax.random.fold_in(own_key, 6), dim), (blocks,), jnp.float32, smallest / len(pieces), high / len(pieces))
        return jnp.repeat(jnp.exp(draws), extent[dim] // blocks).reshape((-1,) + (1,) * (len(extent) - dim - 1))

    level = one(*pieces[0])
    for cut in pieces[1:]:
        level = level * one(*cut)
    return level


def noise(stream_key, dims, deviation, reach, cuts=(), held_as=jnp.bfloat16):
    factor_of = block_levels(stream_key, dims, cuts, -0.22, 0.18) if cuts else 1.0
    values = jax.random.normal(stream_key, dims, jnp.float32) * deviation * factor_of
    return jnp.minimum(jnp.maximum(values, -reach), reach).astype(held_as)


def setup_inputs(seed: int = 0) -> dict:
    streams_of = jax.random.split(jax.random.key(seed), 8)
    displacement = noise(streams_of[0], (3, NX, NY, NZ), 0.2, 3.0, ((1, 8), (2, 4), (3, 8)), jnp.float32)
    velocity = noise(streams_of[1], (3, NX, NY, NZ), 1.0, 6.0, ((1, 8), (2, 4), (3, 8)), jnp.float32)
    bulk_modulus = jnp.clip(jnp.exp(math.log(20000.0) - 1.89712 * jax.random.uniform(streams_of[2], (NX, NY, NZ), jnp.float32) ** block_levels(streams_of[2], (NX, NY, NZ), ((0, 8), (1, 4), (2, 8)), -0.2, 0.2)), 3000.0, 20000.0)
    shear_modulus = jnp.clip(jnp.exp(math.log(1500.0) - 1.609438 * jax.random.uniform(streams_of[3], (NX, NY, NZ), jnp.float32) ** block_levels(streams_of[3], (NX, NY, NZ), ((0, 8), (1, 4), (2, 8)), -0.2, 0.2)), 300.0, 1500.0)
    blast_load = jnp.clip(jax.random.uniform(streams_of[4], (3, NX, NY, NZ), jnp.float32, -50.0, 50.0) * block_levels(streams_of[4], (3, NX, NY, NZ), ((1, 8), (2, 4), (3, 8)), -0.4, 0.0), -50.0, 50.0)
    loaded = place_ends((jax.random.randint(streams_of[5], (NX, NY, NZ), 0, 4) < 1).astype(jnp.int32), jax.random.fold_in(streams_of[5], 1), 0, 1)
    broken = draw_broken(jax.random.fold_in(streams_of[7], 71), 0)
    return {"displacement": displacement, "velocity": velocity, "bulk_modulus": bulk_modulus, "shear_modulus": shear_modulus, "blast_load": blast_load, "loaded": loaded, "broken": broken}


TIME_STEP = 0.01

def offset_table():
    forward = []
    for step_x in range(-3, 4):
        for step_y in range(-3, 4):
            for step_z in range(-3, 4):
                squared = step_x * step_x + step_y * step_y + step_z * step_z
                if squared == 0 or squared > 9:
                    continue
                summed = step_x + step_y + step_z
                if summed > 0 or (summed == 0 and (step_x > 0 or (step_x == 0 and step_y > 0))):
                    forward.append((step_x, step_y, step_z))
    backward = []
    for entry in forward:
        backward.append((-entry[0], -entry[1], -entry[2]))
    return forward + backward

def reference(displacement, velocity, bulk_modulus, shear_modulus, blast_load, loaded, broken):
    offset_rows = jnp.asarray(np.array(offset_table(), dtype=np.int32))
    offset_float = offset_rows.astype(jnp.float32)
    lengths = jnp.sqrt(lax.optimization_barrier(jnp.sum(offset_float * offset_float, axis=1)))
    grid_shape = displacement.shape[1:]
    inside = jnp.pad(jnp.ones(grid_shape, jnp.float32), 3)

    def window(padded, number):
        lead = padded.ndim - 3
        starts = [jnp.int32(0)] * lead + [jnp.int32(3) + offset_rows[number, 0], jnp.int32(3) + offset_rows[number, 1], jnp.int32(3) + offset_rows[number, 2]]
        return lax.dynamic_slice(padded, starts, tuple(padded.shape[:lead]) + tuple(grid_shape))

    def intact(number):
        packed_word = lax.dynamic_index_in_dim(broken, number // 8, 0, keepdims=False)
        bit_value = packed_word // jnp.power(jnp.int32(2), number % 8) % 2
        return window(inside, number) * (1.0 - bit_value.astype(jnp.float32))

    def add_volume(number, running):
        return running + window(inside, number) * lengths[number] * lengths[number]
    weight = lax.fori_loop(0, 122, add_volume, jnp.zeros(grid_shape, jnp.float32))
    stiffness = 15.0 * shear_modulus / weight
    padded_stiffness = jnp.pad(stiffness, 3)
    load_force = loaded.astype(jnp.float32)[None] * blast_load
    displacement_now = displacement
    velocity_now = velocity
    for step_index in range(STEPS):
        padded_disp = jnp.pad(displacement_now, ((0, 0), (3, 3), (3, 3), (3, 3)))

        def stretch(number):
            difference = window(padded_disp, number) - displacement_now + offset_float[number][:, None, None, None]
            return jnp.sqrt(lax.optimization_barrier(jnp.sum(difference * difference, axis=0))) - lengths[number]

        def add_dilatation(number, running):
            return running + intact(number) * lengths[number] * stretch(number)
        dilatation = 3.0 * lax.fori_loop(0, 122, add_dilatation, jnp.zeros(grid_shape, jnp.float32)) / weight
        coupling = dilatation * (3.0 * bulk_modulus - 5.0 * shear_modulus) / weight
        padded_coupling = jnp.pad(coupling, 3)

        def add_force(number, running):
            scalar = intact(number) * (lengths[number] * (coupling + window(padded_coupling, number)) + (stiffness + window(padded_stiffness, number)) * stretch(number))
            return running + scalar[None] * (offset_float[number] / lengths[number])[:, None, None, None]
        force_sum = lax.fori_loop(0, 122, add_force, jnp.zeros((3,) + tuple(grid_shape), jnp.float32))
        velocity_now = velocity_now + TIME_STEP * (force_sum + load_force)
        displacement_now = displacement_now + TIME_STEP * velocity_now
    return (displacement_now, velocity_now)
```

```python
import math

import jax
import jax.numpy as jnp
from jax import lax
from jax.sharding import PartitionSpec as P

STEPS = 2


TIME_STEP = 0.01


def extended_2(cells, sides, width):
    for axis, dim in sides:
        count = lax.axis_size(axis)
        ends = count - 1
        head = lax.slice_in_dim(cells, 0, width, axis=dim)
        tail = lax.slice_in_dim(cells, cells.shape[dim] - width, cells.shape[dim], axis=dim)
        cells = jnp.concatenate(
            [
                lax.ppermute(tail, axis, [(i, (i + 1) % count) for i in range(ends)]),
                cells,
                lax.ppermute(head, axis, [((i + 1) % count, i) for i in range(ends)]),
            ],
            axis=dim,
        )
    return cells


def offset_table():
    forward = []
    for step_x in range(-3, 4):
        for step_y in range(-3, 4):
            for step_z in range(-3, 4):
                squared = step_x * step_x + step_y * step_y + step_z * step_z
                if squared == 0 or squared > 9:
                    continue
                summed = step_x + step_y + step_z
                if summed > 0 or (summed == 0 and (step_x > 0 or (step_x == 0 and step_y > 0))):
                    forward.append((step_x, step_y, step_z))
    backward = []
    for entry in forward:
        backward.append((-entry[0], -entry[1], -entry[2]))
    return forward + backward


def presence(cell_count, device_index, device_count, offset_value):
    position = device_index * cell_count + jnp.arange(cell_count, dtype=jnp.int32) + offset_value
    return ((position >= 0) & (position < device_count * cell_count)).astype(jnp.float32)


def target_slices(entry, cell_shape):
    return (
        slice(3 + entry[0], 3 + entry[0] + cell_shape[0]),
        slice(3 + entry[1], 3 + entry[1] + cell_shape[1]),
        slice(3 + entry[2], 3 + entry[2] + cell_shape[2]),
    )


def window(padded, entry, cell_shape):
    leading = tuple((slice(None) for position in range(padded.ndim - 3)))
    return padded[leading + target_slices(entry, cell_shape)]


def extend(values):
    return extended_2(values, (("gx", 1), ("gy", 2), ("gz", 3)), 3)


def local(displacement, velocity, bulk_modulus, shear_modulus, blast_load, loaded, broken):
    offsets = offset_table()
    count = len(offsets)
    cell_shape = displacement.shape[1:]
    cells_x, cells_y, cells_z = cell_shape
    index_x = lax.axis_index("gx")
    index_y = lax.axis_index("gy")
    index_z = lax.axis_index("gz")
    span_x = lax.axis_size("gx")
    span_y = lax.axis_size("gy")
    span_z = lax.axis_size("gz")
    along_x = {value: presence(cells_x, index_x, span_x, value) for value in range(-3, 4)}
    along_y = {value: presence(cells_y, index_y, span_y, value) for value in range(-3, 4)}
    along_z = {value: presence(cells_z, index_z, span_z, value) for value in range(-3, 4)}
    lengths = [math.sqrt(entry[0] ** 2 + entry[1] ** 2 + entry[2] ** 2) for entry in offsets]
    directions = [
        jnp.array(
            [entry[0] / lengths[number], entry[1] / lengths[number], entry[2] / lengths[number]],
            jnp.float32,
        )[:, None, None, None]
        for number, entry in enumerate(offsets)
    ]
    weight = jnp.zeros(cell_shape, jnp.float32)
    intacts = []
    for number in range(count):
        entry = offsets[number]
        exists = (
            along_x[entry[0]][:, None, None]
            * along_y[entry[1]][None, :, None]
            * along_z[entry[2]][None, None, :]
        )
        weight = weight + exists * (lengths[number] * lengths[number])
        bit_value = broken[number // 8] // 2 ** (number % 8) % 2
        intacts.append(exists * (1.0 - bit_value.astype(jnp.float32)))
    stiffness = 15.0 * shear_modulus / weight
    load_force = loaded.astype(jnp.float32)[None] * blast_load
    modulus_factor = 3.0 * bulk_modulus - 5.0 * shear_modulus
    displacement_now = displacement
    velocity_now = velocity
    padded_stiffness = None
    for step_index in range(STEPS):
        if step_index == 0:
            extended = extend(jnp.concatenate([displacement_now, stiffness[None]], axis=0))
            padded_stiffness = extended[3]
        else:
            extended = extend(displacement_now)
        padded_disp = extended[:3]

        def stretch(number):
            entry = offsets[number]
            difference = (
                window(padded_disp, entry, cell_shape)
                - displacement_now
                + jnp.array(entry, jnp.float32)[:, None, None, None]
            )
            return jnp.sqrt(jnp.sum(difference * difference, axis=0)) - lengths[number]

        stretches = [stretch(number) for number in range(count)]
        bond_sum = jnp.zeros(cell_shape, jnp.float32)
        for number in range(count):
            bond_sum = bond_sum + intacts[number] * lengths[number] * stretches[number]
        dilatation = 3.0 * bond_sum / weight
        coupling = dilatation * modulus_factor / weight
        padded_coupling = extended_2(coupling, (("gx", 0), ("gy", 1), ("gz", 2)), 3)
        force_sum = jnp.zeros((3,) + tuple(cell_shape), jnp.float32)
        for number in range(count):
            entry = offsets[number]
            scalar = intacts[number] * (
                lengths[number] * (coupling + window(padded_coupling, entry, cell_shape))
                + (stiffness + window(padded_stiffness, entry, cell_shape)) * stretches[number]
            )
            force_sum = force_sum + scalar[None] * directions[number]
        velocity_now = velocity_now + TIME_STEP * (force_sum + load_force)
        displacement_now = displacement_now + TIME_STEP * velocity_now
    return (displacement_now, velocity_now)


def solution(mesh):
    placed = (
        P(None, "gx", "gy", "gz"),
        P(None, "gx", "gy", "gz"),
        P("gx", "gy", "gz"),
        P("gx", "gy", "gz"),
        P(None, "gx", "gy", "gz"),
        P("gx", "gy", "gz"),
        P(None, "gx", "gy", "gz"),
    )
    return jax.shard_map(
        local,
        mesh=mesh,
        in_specs=placed,
        out_specs=(P(None, "gx", "gy", "gz"), P(None, "gx", "gy", "gz")),
        check_vma=False,
    )
```

```python
import math

import jax
import jax.numpy as jnp
from jax import lax
from jax.experimental import pallas as pl
from jax.experimental.pallas import tpu as pltpu
from jax.sharding import PartitionSpec as P

STEPS = 2


TIME_STEP = 0.01

INTERPRET = False

ROWS = 4


def extended_2(cells, sides, width):
    for axis, dim in sides:
        count = lax.axis_size(axis)
        ends = count - 1
        head = lax.slice_in_dim(cells, 0, width, axis=dim)
        tail = lax.slice_in_dim(cells, cells.shape[dim] - width, cells.shape[dim], axis=dim)
        cells = jnp.concatenate(
            [
                lax.ppermute(tail, axis, [(i, (i + 1) % count) for i in range(ends)]),
                cells,
                lax.ppermute(head, axis, [((i + 1) % count, i) for i in range(ends)]),
            ],
            axis=dim,
        )
    return cells


def offset_table():
    forward = []
    for step_x in range(-3, 4):
        for step_y in range(-3, 4):
            for step_z in range(-3, 4):
                squared = step_x * step_x + step_y * step_y + step_z * step_z
                if squared == 0 or squared > 9:
                    continue
                summed = step_x + step_y + step_z
                if summed > 0 or (summed == 0 and (step_x > 0 or (step_x == 0 and step_y > 0))):
                    forward.append((step_x, step_y, step_z))
    backward = []
    for entry in forward:
        backward.append((-entry[0], -entry[1], -entry[2]))
    return forward + backward


OFFSETS = offset_table()
LENGTHS = [math.sqrt(e[0] ** 2 + e[1] ** 2 + e[2] ** 2) for e in OFFSETS]
PAIRS = sorted({(e[1], e[2]) for e in OFFSETS} | {(0, 0)})
PAIR_OF = {pair: number for number, pair in enumerate(PAIRS)}


def presence(cell_count, device_index, device_count, offset_value):
    position = device_index * cell_count + jnp.arange(cell_count, dtype=jnp.int32) + offset_value
    return ((position >= 0) & (position < device_count * cell_count)).astype(jnp.float32)


def extend(values):
    return extended_2(values, (("gx", 1), ("gy", 2), ("gz", 3)), 3)


def shifted(padded, cells_y, cells_z):
    return jnp.stack(
        [padded[..., 3 + oy:3 + oy + cells_y, 3 + oz:3 + oz + cells_z] for (oy, oz) in PAIRS], axis=0
    )


def stretch_kernel(us_ref, intact_ref, weight_ref, factor_ref, stretch_ref, coupling_ref):
    centre = PAIR_OF[(0, 0)]
    blocks = weight_ref.shape[0] // ROWS

    def body(block, carry):
        x0 = pl.multiple_of(block * ROWS, ROWS)
        own = [us_ref[centre, c, pl.ds(x0 + 3, ROWS)] for c in range(3)]
        total = jnp.zeros_like(own[0])
        for number, entry in enumerate(OFFSETS):
            pair = PAIR_OF[(entry[1], entry[2])]
            squared = None
            for c in range(3):
                diff = us_ref[pair, c, pl.ds(x0 + 3 + entry[0], ROWS)] - own[c]
                if entry[c] != 0:
                    diff = diff + float(entry[c])
                squared = diff * diff if squared is None else squared + diff * diff
            value = jnp.sqrt(squared) - LENGTHS[number]
            stretch_ref[number, pl.ds(x0, ROWS)] = value
            total = total + intact_ref[number, pl.ds(x0, ROWS)] * LENGTHS[number] * value
        weight = weight_ref[pl.ds(x0, ROWS)]
        dilatation = 3.0 * total / weight
        coupling_ref[pl.ds(x0, ROWS)] = dilatation * factor_ref[pl.ds(x0, ROWS)] / weight
        return carry

    lax.fori_loop(0, blocks, body, 0)


def force_kernel(cs_ref, ss_ref, stretch_ref, intact_ref, u_ref, v_ref, load_ref, unew_ref, vnew_ref):
    centre = PAIR_OF[(0, 0)]
    blocks = u_ref.shape[1] // ROWS

    def body(block, carry):
        x0 = pl.multiple_of(block * ROWS, ROWS)
        c_own = cs_ref[centre, pl.ds(x0 + 3, ROWS)]
        s_own = ss_ref[centre, pl.ds(x0 + 3, ROWS)]
        force = [None, None, None]
        for number, entry in enumerate(OFFSETS):
            pair = PAIR_OF[(entry[1], entry[2])]
            rows = pl.ds(x0 + 3 + entry[0], ROWS)
            scalar = intact_ref[number, pl.ds(x0, ROWS)] * (
                LENGTHS[number] * (c_own + cs_ref[pair, rows])
                + (s_own + ss_ref[pair, rows]) * stretch_ref[number, pl.ds(x0, ROWS)]
            )
            for c in range(3):
                if entry[c] != 0:
                    term = scalar * (entry[c] / LENGTHS[number])
                    force[c] = term if force[c] is None else force[c] + term
        for c in range(3):
            v_new = v_ref[c, pl.ds(x0, ROWS)] + TIME_STEP * (force[c] + load_ref[c, pl.ds(x0, ROWS)])
            vnew_ref[c, pl.ds(x0, ROWS)] = v_new
            unew_ref[c, pl.ds(x0, ROWS)] = u_ref[c, pl.ds(x0, ROWS)] + TIME_STEP * v_new
        return carry

    lax.fori_loop(0, blocks, body, 0)


def compiler_params():
    return pltpu.CompilerParams(vmem_limit_bytes=100 * 1024 * 1024)


def local(displacement, velocity, bulk_modulus, shear_modulus, blast_load, loaded, broken):
    count = len(OFFSETS)
    cell_shape = displacement.shape[1:]
    cells_x, cells_y, cells_z = cell_shape
    index_x = lax.axis_index("gx")
    index_y = lax.axis_index("gy")
    index_z = lax.axis_index("gz")
    span_x = lax.axis_size("gx")
    span_y = lax.axis_size("gy")
    span_z = lax.axis_size("gz")
    along_x = {value: presence(cells_x, index_x, span_x, value) for value in range(-3, 4)}
    along_y = {value: presence(cells_y, index_y, span_y, value) for value in range(-3, 4)}
    along_z = {value: presence(cells_z, index_z, span_z, value) for value in range(-3, 4)}
    exists_x = jnp.stack([along_x[e[0]] for e in OFFSETS])
    exists_y = jnp.stack([along_y[e[1]] for e in OFFSETS])
    exists_z = jnp.stack([along_z[e[2]] for e in OFFSETS])
    exists = exists_x[:, :, None, None] * exists_y[:, None, :, None] * exists_z[:, None, None, :]
    squares = jnp.array([l * l for l in LENGTHS], jnp.float32)
    weight = jnp.sum(exists * squares[:, None, None, None], axis=0)
    shifts = jnp.arange(8, dtype=jnp.int32)
    bits = jnp.right_shift(broken[:, None], shifts[None, :, None, None, None]) & 1
    bits = bits.reshape((broken.shape[0] * 8,) + tuple(cell_shape))[:count]
    intact = exists * (1.0 - bits.astype(jnp.float32))
    stiffness = 15.0 * shear_modulus / weight
    load_force = loaded.astype(jnp.float32)[None] * blast_load
    modulus_factor = 3.0 * bulk_modulus - 5.0 * shear_modulus
    displacement_now = displacement
    velocity_now = velocity
    shifted_stiffness = None
    f32 = jnp.float32
    for step_index in range(STEPS):
        if step_index == 0:
            extended = extend(jnp.concatenate([displacement_now, stiffness[None]], axis=0))
            shifted_stiffness = shifted(extended[3], cells_y, cells_z)
        else:
            extended = extend(displacement_now)
        shifted_disp = shifted(extended[:3], cells_y, cells_z)
        stretches, coupling = pl.pallas_call(
            stretch_kernel,
            out_shape=(
                jax.ShapeDtypeStruct((count,) + tuple(cell_shape), f32),
                jax.ShapeDtypeStruct(tuple(cell_shape), f32),
            ),
            compiler_params=compiler_params(),
            interpret=INTERPRET,
        )(shifted_disp, intact, weight, modulus_factor)
        padded_coupling = extended_2(coupling, (("gx", 0), ("gy", 1), ("gz", 2)), 3)
        shifted_coupling = shifted(padded_coupling, cells_y, cells_z)
        displacement_now, velocity_now = pl.pallas_call(
            force_kernel,
            out_shape=(
                jax.ShapeDtypeStruct(displacement.shape, f32),
                jax.ShapeDtypeStruct(displacement.shape, f32),
            ),
            compiler_params=compiler_params(),
            interpret=INTERPRET,
        )(shifted_coupling, shifted_stiffness, stretches, intact, displacement_now, velocity_now, load_force)
    return (displacement_now, velocity_now)


def solution(mesh):
    placed = (
        P(None, "gx", "gy", "gz"),
        P(None, "gx", "gy", "gz"),
        P("gx", "gy", "gz"),
        P("gx", "gy", "gz"),
        P(None, "gx", "gy", "gz"),
        P("gx", "gy", "gz"),
        P(None, "gx", "gy", "gz"),
    )
    return jax.shard_map(
        local,
        mesh=mesh,
        in_specs=placed,
        out_specs=(P(None, "gx", "gy", "gz"), P(None, "gx", "gy", "gz")),
        check_vma=False,
    )
```

```python
import math

import jax
import jax.numpy as jnp
from jax import lax
from jax.experimental import pallas as pl
from jax.experimental.pallas import tpu as pltpu
from jax.sharding import PartitionSpec as P

STEPS = 2


TIME_STEP = 0.01

INTERPRET = False

ROWS = 4


def extended_2(cells, sides, width):
    for axis, dim in sides:
        count = lax.axis_size(axis)
        ends = count - 1
        head = lax.slice_in_dim(cells, 0, width, axis=dim)
        tail = lax.slice_in_dim(cells, cells.shape[dim] - width, cells.shape[dim], axis=dim)
        cells = jnp.concatenate(
            [
                lax.ppermute(tail, axis, [(i, (i + 1) % count) for i in range(ends)]),
                cells,
                lax.ppermute(head, axis, [((i + 1) % count, i) for i in range(ends)]),
            ],
            axis=dim,
        )
    return cells


def offset_table():
    forward = []
    for step_x in range(-3, 4):
        for step_y in range(-3, 4):
            for step_z in range(-3, 4):
                squared = step_x * step_x + step_y * step_y + step_z * step_z
                if squared == 0 or squared > 9:
                    continue
                summed = step_x + step_y + step_z
                if summed > 0 or (summed == 0 and (step_x > 0 or (step_x == 0 and step_y > 0))):
                    forward.append((step_x, step_y, step_z))
    backward = []
    for entry in forward:
        backward.append((-entry[0], -entry[1], -entry[2]))
    return forward + backward


OFFSETS = offset_table()
LENGTHS = [math.sqrt(e[0] ** 2 + e[1] ** 2 + e[2] ** 2) for e in OFFSETS]
PAIRS = sorted({(e[1], e[2]) for e in OFFSETS} | {(0, 0)})
PAIR_OF = {pair: number for number, pair in enumerate(PAIRS)}


def presence(cell_count, device_index, device_count, offset_value):
    position = device_index * cell_count + jnp.arange(cell_count, dtype=jnp.int32) + offset_value
    return ((position >= 0) & (position < device_count * cell_count)).astype(jnp.float32)


def extend(values):
    return extended_2(values, (("gx", 1), ("gy", 2), ("gz", 3)), 3)


def fill_stack(stack_ref, padded_ref, leading):
    cells_y, cells_z = stack_ref.shape[-2], stack_ref.shape[-1]
    for pair, (oy, oz) in enumerate(PAIRS):
        for c in leading:
            index = (pair,) if c is None else (pair, c)
            source = (slice(None),) if c is None else (c, slice(None))
            stack_ref[index] = padded_ref[source + (pl.ds(3 + oy, cells_y), pl.ds(3 + oz, cells_z))]


def stretch_kernel(ext_ref, intact_ref, weight_ref, factor_ref, stretch_ref, coupling_ref, us_ref):
    fill_stack(us_ref, ext_ref, (0, 1, 2))
    centre = PAIR_OF[(0, 0)]
    blocks = weight_ref.shape[0] // ROWS

    def body(block, carry):
        x0 = pl.multiple_of(block * ROWS, ROWS)
        own = [us_ref[centre, c, pl.ds(x0 + 3, ROWS)] for c in range(3)]
        total = jnp.zeros_like(own[0])
        for number, entry in enumerate(OFFSETS):
            pair = PAIR_OF[(entry[1], entry[2])]
            squared = None
            for c in range(3):
                diff = us_ref[pair, c, pl.ds(x0 + 3 + entry[0], ROWS)] - own[c]
                if entry[c] != 0:
                    diff = diff + float(entry[c])
                squared = diff * diff if squared is None else squared + diff * diff
            value = jnp.sqrt(squared) - LENGTHS[number]
            stretch_ref[number, pl.ds(x0, ROWS)] = value
            total = total + intact_ref[number, pl.ds(x0, ROWS)] * LENGTHS[number] * value
        weight = weight_ref[pl.ds(x0, ROWS)]
        dilatation = 3.0 * total / weight
        coupling_ref[pl.ds(x0, ROWS)] = dilatation * factor_ref[pl.ds(x0, ROWS)] / weight
        return carry

    lax.fori_loop(0, blocks, body, 0)


def force_kernel(pc_ref, ps_ref, stretch_ref, intact_ref, u_ref, v_ref, load_ref, unew_ref, vnew_ref, cs_ref, ss_ref):
    fill_stack(cs_ref, pc_ref, (None,))
    fill_stack(ss_ref, ps_ref, (None,))
    centre = PAIR_OF[(0, 0)]
    blocks = u_ref.shape[1] // ROWS

    def body(block, carry):
        x0 = pl.multiple_of(block * ROWS, ROWS)
        c_own = cs_ref[centre, pl.ds(x0 + 3, ROWS)]
        s_own = ss_ref[centre, pl.ds(x0 + 3, ROWS)]
        force = [None, None, None]
        for number, entry in enumerate(OFFSETS):
            pair = PAIR_OF[(entry[1], entry[2])]
            rows = pl.ds(x0 + 3 + entry[0], ROWS)
            scalar = intact_ref[number, pl.ds(x0, ROWS)] * (
                LENGTHS[number] * (c_own + cs_ref[pair, rows])
                + (s_own + ss_ref[pair, rows]) * stretch_ref[number, pl.ds(x0, ROWS)]
            )
            for c in range(3):
                if entry[c] != 0:
                    term = scalar * (entry[c] / LENGTHS[number])
                    force[c] = term if force[c] is None else force[c] + term
        for c in range(3):
            v_new = v_ref[c, pl.ds(x0, ROWS)] + TIME_STEP * (force[c] + load_ref[c, pl.ds(x0, ROWS)])
            vnew_ref[c, pl.ds(x0, ROWS)] = v_new
            unew_ref[c, pl.ds(x0, ROWS)] = u_ref[c, pl.ds(x0, ROWS)] + TIME_STEP * v_new
        return carry

    lax.fori_loop(0, blocks, body, 0)


def compiler_params():
    return pltpu.CompilerParams(vmem_limit_bytes=100 * 1024 * 1024)


def local(displacement, velocity, bulk_modulus, shear_modulus, blast_load, loaded, broken):
    count = len(OFFSETS)
    cell_shape = displacement.shape[1:]
    cells_x, cells_y, cells_z = cell_shape
    index_x = lax.axis_index("gx")
    index_y = lax.axis_index("gy")
    index_z = lax.axis_index("gz")
    span_x = lax.axis_size("gx")
    span_y = lax.axis_size("gy")
    span_z = lax.axis_size("gz")
    along_x = {value: presence(cells_x, index_x, span_x, value) for value in range(-3, 4)}
    along_y = {value: presence(cells_y, index_y, span_y, value) for value in range(-3, 4)}
    along_z = {value: presence(cells_z, index_z, span_z, value) for value in range(-3, 4)}
    exists_x = jnp.stack([along_x[e[0]] for e in OFFSETS])
    exists_y = jnp.stack([along_y[e[1]] for e in OFFSETS])
    exists_z = jnp.stack([along_z[e[2]] for e in OFFSETS])
    exists = exists_x[:, :, None, None] * exists_y[:, None, :, None] * exists_z[:, None, None, :]
    squares = jnp.array([l * l for l in LENGTHS], jnp.float32)
    weight = jnp.sum(exists * squares[:, None, None, None], axis=0)
    shifts = jnp.arange(8, dtype=jnp.int32)
    bits = jnp.right_shift(broken[:, None], shifts[None, :, None, None, None]) & 1
    bits = bits.reshape((broken.shape[0] * 8,) + tuple(cell_shape))[:count]
    intact = exists * (1.0 - bits.astype(jnp.float32))
    stiffness = 15.0 * shear_modulus / weight
    load_force = loaded.astype(jnp.float32)[None] * blast_load
    modulus_factor = 3.0 * bulk_modulus - 5.0 * shear_modulus
    displacement_now = displacement
    velocity_now = velocity
    padded_stiffness = None
    f32 = jnp.float32
    pairs = len(PAIRS)
    halo_x = cells_x + 6
    for step_index in range(STEPS):
        if step_index == 0:
            extended = extend(jnp.concatenate([displacement_now, stiffness[None]], axis=0))
            padded_stiffness = extended[3]
        else:
            extended = extend(displacement_now)
        stretches, coupling = pl.pallas_call(
            stretch_kernel,
            out_shape=(
                jax.ShapeDtypeStruct((count,) + tuple(cell_shape), f32),
                jax.ShapeDtypeStruct(tuple(cell_shape), f32),
            ),
            scratch_shapes=[pltpu.VMEM((pairs, 3, halo_x, cells_y, cells_z), f32)],
            compiler_params=compiler_params(),
            interpret=INTERPRET,
        )(extended[:3], intact, weight, modulus_factor)
        padded_coupling = extended_2(coupling, (("gx", 0), ("gy", 1), ("gz", 2)), 3)
        displacement_now, velocity_now = pl.pallas_call(
            force_kernel,
            out_shape=(
                jax.ShapeDtypeStruct(displacement.shape, f32),
                jax.ShapeDtypeStruct(displacement.shape, f32),
            ),
            scratch_shapes=[
                pltpu.VMEM((pairs, halo_x, cells_y, cells_z), f32),
                pltpu.VMEM((pairs, halo_x, cells_y, cells_z), f32),
            ],
            compiler_params=compiler_params(),
            interpret=INTERPRET,
        )(padded_coupling, padded_stiffness, stretches, intact, displacement_now, velocity_now, load_force)
    return (displacement_now, velocity_now)


def solution(mesh):
    placed = (
        P(None, "gx", "gy", "gz"),
        P(None, "gx", "gy", "gz"),
        P("gx", "gy", "gz"),
        P("gx", "gy", "gz"),
        P(None, "gx", "gy", "gz"),
        P("gx", "gy", "gz"),
        P(None, "gx", "gy", "gz"),
    )
    return jax.shard_map(
        local,
        mesh=mesh,
        in_specs=placed,
        out_specs=(P(None, "gx", "gy", "gz"), P(None, "gx", "gy", "gz")),
        check_vma=False,
    )
```

```python
import math

import jax
import jax.numpy as jnp
from jax import lax
from jax.experimental import pallas as pl
from jax.experimental.pallas import tpu as pltpu
from jax.sharding import PartitionSpec as P

STEPS = 2


TIME_STEP = 0.01

INTERPRET = False

ROWS = 4


def extended_2(cells, sides, width):
    for axis, dim in sides:
        count = lax.axis_size(axis)
        ends = count - 1
        head = lax.slice_in_dim(cells, 0, width, axis=dim)
        tail = lax.slice_in_dim(cells, cells.shape[dim] - width, cells.shape[dim], axis=dim)
        cells = jnp.concatenate(
            [
                lax.ppermute(tail, axis, [(i, (i + 1) % count) for i in range(ends)]),
                cells,
                lax.ppermute(head, axis, [((i + 1) % count, i) for i in range(ends)]),
            ],
            axis=dim,
        )
    return cells


def offset_table():
    forward = []
    for step_x in range(-3, 4):
        for step_y in range(-3, 4):
            for step_z in range(-3, 4):
                squared = step_x * step_x + step_y * step_y + step_z * step_z
                if squared == 0 or squared > 9:
                    continue
                summed = step_x + step_y + step_z
                if summed > 0 or (summed == 0 and (step_x > 0 or (step_x == 0 and step_y > 0))):
                    forward.append((step_x, step_y, step_z))
    backward = []
    for entry in forward:
        backward.append((-entry[0], -entry[1], -entry[2]))
    return forward + backward


OFFSETS = offset_table()
LENGTHS = [math.sqrt(e[0] ** 2 + e[1] ** 2 + e[2] ** 2) for e in OFFSETS]
PAIRS = sorted({(e[1], e[2]) for e in OFFSETS} | {(0, 0)})
PAIR_OF = {pair: number for number, pair in enumerate(PAIRS)}


def presence(cell_count, device_index, device_count, offset_value):
    position = device_index * cell_count + jnp.arange(cell_count, dtype=jnp.int32) + offset_value
    return ((position >= 0) & (position < device_count * cell_count)).astype(jnp.float32)


def extend(values):
    return extended_2(values, (("gx", 1), ("gy", 2), ("gz", 3)), 3)


def fill_stack(stack_ref, padded_ref, leading):
    cells_y, cells_z = stack_ref.shape[-2], stack_ref.shape[-1]
    for pair, (oy, oz) in enumerate(PAIRS):
        for c in leading:
            index = (pair,) if c is None else (pair, c)
            source = (slice(None),) if c is None else (c, slice(None))
            stack_ref[index] = padded_ref[source + (pl.ds(3 + oy, cells_y), pl.ds(3 + oz, cells_z))]


def stretch_kernel(ext_ref, intact_ref, weight_ref, factor_ref, stretch_ref, coupling_ref, us_ref):
    block = pl.program_id(0)

    @pl.when(block == 0)
    def _():
        fill_stack(us_ref, ext_ref, (0, 1, 2))

    centre = PAIR_OF[(0, 0)]
    x0 = pl.multiple_of(block * ROWS, ROWS)
    own = [us_ref[centre, c, pl.ds(x0 + 3, ROWS)] for c in range(3)]
    total = jnp.zeros_like(own[0])
    for number, entry in enumerate(OFFSETS):
        pair = PAIR_OF[(entry[1], entry[2])]
        squared = None
        for c in range(3):
            diff = us_ref[pair, c, pl.ds(x0 + 3 + entry[0], ROWS)] - own[c]
            if entry[c] != 0:
                diff = diff + float(entry[c])
            squared = diff * diff if squared is None else squared + diff * diff
        value = jnp.sqrt(squared) - LENGTHS[number]
        stretch_ref[number] = value
        total = total + intact_ref[number] * LENGTHS[number] * value
    weight = weight_ref[...]
    dilatation = 3.0 * total / weight
    coupling_ref[...] = dilatation * factor_ref[...] / weight


def force_kernel(pc_ref, ps_ref, stretch_ref, intact_ref, u_ref, v_ref, load_ref, unew_ref, vnew_ref, cs_ref, ss_ref):
    block = pl.program_id(0)

    @pl.when(block == 0)
    def _():
        fill_stack(cs_ref, pc_ref, (None,))
        fill_stack(ss_ref, ps_ref, (None,))

    centre = PAIR_OF[(0, 0)]
    x0 = pl.multiple_of(block * ROWS, ROWS)
    c_own = cs_ref[centre, pl.ds(x0 + 3, ROWS)]
    s_own = ss_ref[centre, pl.ds(x0 + 3, ROWS)]
    force = [None, None, None]
    for number, entry in enumerate(OFFSETS):
        pair = PAIR_OF[(entry[1], entry[2])]
        rows = pl.ds(x0 + 3 + entry[0], ROWS)
        scalar = intact_ref[number] * (
            LENGTHS[number] * (c_own + cs_ref[pair, rows])
            + (s_own + ss_ref[pair, rows]) * stretch_ref[number]
        )
        for c in range(3):
            if entry[c] != 0:
                term = scalar * (entry[c] / LENGTHS[number])
                force[c] = term if force[c] is None else force[c] + term
    for c in range(3):
        v_new = v_ref[c] + TIME_STEP * (force[c] + load_ref[c])
        vnew_ref[c] = v_new
        unew_ref[c] = u_ref[c] + TIME_STEP * v_new


def compiler_params():
    return pltpu.CompilerParams(vmem_limit_bytes=100 * 1024 * 1024)


def local(displacement, velocity, bulk_modulus, shear_modulus, blast_load, loaded, broken):
    count = len(OFFSETS)
    cell_shape = displacement.shape[1:]
    cells_x, cells_y, cells_z = cell_shape
    index_x = lax.axis_index("gx")
    index_y = lax.axis_index("gy")
    index_z = lax.axis_index("gz")
    span_x = lax.axis_size("gx")
    span_y = lax.axis_size("gy")
    span_z = lax.axis_size("gz")
    along_x = {value: presence(cells_x, index_x, span_x, value) for value in range(-3, 4)}
    along_y = {value: presence(cells_y, index_y, span_y, value) for value in range(-3, 4)}
    along_z = {value: presence(cells_z, index_z, span_z, value) for value in range(-3, 4)}
    exists_x = jnp.stack([along_x[e[0]] for e in OFFSETS])
    exists_y = jnp.stack([along_y[e[1]] for e in OFFSETS])
    exists_z = jnp.stack([along_z[e[2]] for e in OFFSETS])
    exists = exists_x[:, :, None, None] * exists_y[:, None, :, None] * exists_z[:, None, None, :]
    squares = jnp.array([l * l for l in LENGTHS], jnp.float32)
    weight = jnp.sum(exists * squares[:, None, None, None], axis=0)
    shifts = jnp.arange(8, dtype=jnp.int32)
    bits = jnp.right_shift(broken[:, None], shifts[None, :, None, None, None]) & 1
    bits = bits.reshape((broken.shape[0] * 8,) + tuple(cell_shape))[:count]
    intact = exists * (1.0 - bits.astype(jnp.float32))
    stiffness = 15.0 * shear_modulus / weight
    load_force = loaded.astype(jnp.float32)[None] * blast_load
    modulus_factor = 3.0 * bulk_modulus - 5.0 * shear_modulus
    displacement_now = displacement
    velocity_now = velocity
    padded_stiffness = None
    f32 = jnp.float32
    pairs = len(PAIRS)
    halo_x = cells_x + 6

    def whole(shape):
        return pl.BlockSpec(shape, lambda block: (0,) * len(shape))

    bonds_spec = pl.BlockSpec((count, ROWS, cells_y, cells_z), lambda block: (0, block, 0, 0))
    cells_spec = pl.BlockSpec((ROWS, cells_y, cells_z), lambda block: (block, 0, 0))
    vector_spec = pl.BlockSpec((3, ROWS, cells_y, cells_z), lambda block: (0, block, 0, 0))
    for step_index in range(STEPS):
        if step_index == 0:
            extended = extend(jnp.concatenate([displacement_now, stiffness[None]], axis=0))
            padded_stiffness = extended[3]
        else:
            extended = extend(displacement_now)
        stretches, coupling = pl.pallas_call(
            stretch_kernel,
            out_shape=(
                jax.ShapeDtypeStruct((count,) + tuple(cell_shape), f32),
                jax.ShapeDtypeStruct(tuple(cell_shape), f32),
            ),
            grid=(cells_x // ROWS,),
            in_specs=[
                whole((3, halo_x, cells_y + 6, cells_z + 6)),
                bonds_spec,
                cells_spec,
                cells_spec,
            ],
            out_specs=(bonds_spec, cells_spec),
            scratch_shapes=[pltpu.VMEM((pairs, 3, halo_x, cells_y, cells_z), f32)],
            compiler_params=compiler_params(),
            interpret=INTERPRET,
        )(extended[:3], intact, weight, modulus_factor)
        padded_coupling = extended_2(coupling, (("gx", 0), ("gy", 1), ("gz", 2)), 3)
        displacement_now, velocity_now = pl.pallas_call(
            force_kernel,
            out_shape=(
                jax.ShapeDtypeStruct(displacement.shape, f32),
                jax.ShapeDtypeStruct(displacement.shape, f32),
            ),
            grid=(cells_x // ROWS,),
            in_specs=[
                whole((halo_x, cells_y + 6, cells_z + 6)),
                whole((halo_x, cells_y + 6, cells_z + 6)),
                bonds_spec,
                bonds_spec,
                vector_spec,
                vector_spec,
                vector_spec,
            ],
            out_specs=(vector_spec, vector_spec),
            scratch_shapes=[
                pltpu.VMEM((pairs, halo_x, cells_y, cells_z), f32),
                pltpu.VMEM((pairs, halo_x, cells_y, cells_z), f32),
            ],
            compiler_params=compiler_params(),
            interpret=INTERPRET,
        )(padded_coupling, padded_stiffness, stretches, intact, displacement_now, velocity_now, load_force)
    return (displacement_now, velocity_now)


def solution(mesh):
    placed = (
        P(None, "gx", "gy", "gz"),
        P(None, "gx", "gy", "gz"),
        P("gx", "gy", "gz"),
        P("gx", "gy", "gz"),
        P(None, "gx", "gy", "gz"),
        P("gx", "gy", "gz"),
        P(None, "gx", "gy", "gz"),
    )
    return jax.shard_map(
        local,
        mesh=mesh,
        in_specs=placed,
        out_specs=(P(None, "gx", "gy", "gz"), P(None, "gx", "gy", "gz")),
        check_vma=False,
    )
```

```python
import math

import jax
import jax.numpy as jnp
from jax import lax
from jax.experimental import pallas as pl
from jax.experimental.pallas import tpu as pltpu
from jax.sharding import PartitionSpec as P

STEPS = 2


TIME_STEP = 0.01

INTERPRET = False

ROWS = 4


def extended_2(cells, sides, width):
    for axis, dim in sides:
        count = lax.axis_size(axis)
        ends = count - 1
        head = lax.slice_in_dim(cells, 0, width, axis=dim)
        tail = lax.slice_in_dim(cells, cells.shape[dim] - width, cells.shape[dim], axis=dim)
        cells = jnp.concatenate(
            [
                lax.ppermute(tail.reshape(-1), axis, [(i, (i + 1) % count) for i in range(ends)]).reshape(tail.shape),
                cells,
                lax.ppermute(head.reshape(-1), axis, [((i + 1) % count, i) for i in range(ends)]).reshape(head.shape),
            ],
            axis=dim,
        )
    return cells


def offset_table():
    forward = []
    for step_x in range(-3, 4):
        for step_y in range(-3, 4):
            for step_z in range(-3, 4):
                squared = step_x * step_x + step_y * step_y + step_z * step_z
                if squared == 0 or squared > 9:
                    continue
                summed = step_x + step_y + step_z
                if summed > 0 or (summed == 0 and (step_x > 0 or (step_x == 0 and step_y > 0))):
                    forward.append((step_x, step_y, step_z))
    backward = []
    for entry in forward:
        backward.append((-entry[0], -entry[1], -entry[2]))
    return forward + backward


OFFSETS = offset_table()
LENGTHS = [math.sqrt(e[0] ** 2 + e[1] ** 2 + e[2] ** 2) for e in OFFSETS]
PAIRS = sorted({(e[1], e[2]) for e in OFFSETS} | {(0, 0)})
PAIR_OF = {pair: number for number, pair in enumerate(PAIRS)}


def presence(cell_count, device_index, device_count, offset_value):
    position = device_index * cell_count + jnp.arange(cell_count, dtype=jnp.int32) + offset_value
    return ((position >= 0) & (position < device_count * cell_count)).astype(jnp.float32)


def extend(values):
    return extended_2(values, (("gx", 1), ("gy", 2), ("gz", 3)), 3)


def fill_stack(stack_ref, padded_ref, leading):
    cells_y, cells_z = stack_ref.shape[-2], stack_ref.shape[-1]
    for pair, (oy, oz) in enumerate(PAIRS):
        for c in leading:
            index = (pair,) if c is None else (pair, c)
            source = (slice(None),) if c is None else (c, slice(None))
            stack_ref[index] = padded_ref[source + (pl.ds(3 + oy, cells_y), pl.ds(3 + oz, cells_z))]


def stretch_kernel(ext_ref, intact_ref, weight_ref, factor_ref, stretch_ref, coupling_ref, us_ref):
    block = pl.program_id(0)

    @pl.when(block == 0)
    def _():
        fill_stack(us_ref, ext_ref, (0, 1, 2))

    centre = PAIR_OF[(0, 0)]
    x0 = pl.multiple_of(block * ROWS, ROWS)
    own = [us_ref[centre, c, pl.ds(x0 + 3, ROWS)] for c in range(3)]
    total = jnp.zeros_like(own[0])
    for number, entry in enumerate(OFFSETS):
        pair = PAIR_OF[(entry[1], entry[2])]
        squared = None
        for c in range(3):
            diff = us_ref[pair, c, pl.ds(x0 + 3 + entry[0], ROWS)] - own[c]
            if entry[c] != 0:
                diff = diff + float(entry[c])
            squared = diff * diff if squared is None else squared + diff * diff
        value = jnp.sqrt(squared) - LENGTHS[number]
        stretch_ref[number] = value
        total = total + intact_ref[number] * LENGTHS[number] * value
    weight = weight_ref[...]
    dilatation = 3.0 * total / weight
    coupling_ref[...] = dilatation * factor_ref[...] / weight


def force_kernel(pc_ref, ps_ref, stretch_ref, intact_ref, u_ref, v_ref, load_ref, unew_ref, vnew_ref, cs_ref, ss_ref):
    block = pl.program_id(0)

    @pl.when(block == 0)
    def _():
        fill_stack(cs_ref, pc_ref, (None,))
        fill_stack(ss_ref, ps_ref, (None,))

    centre = PAIR_OF[(0, 0)]
    x0 = pl.multiple_of(block * ROWS, ROWS)
    c_own = cs_ref[centre, pl.ds(x0 + 3, ROWS)]
    s_own = ss_ref[centre, pl.ds(x0 + 3, ROWS)]
    force = [None, None, None]
    for number, entry in enumerate(OFFSETS):
        pair = PAIR_OF[(entry[1], entry[2])]
        rows = pl.ds(x0 + 3 + entry[0], ROWS)
        scalar = intact_ref[number] * (
            LENGTHS[number] * (c_own + cs_ref[pair, rows])
            + (s_own + ss_ref[pair, rows]) * stretch_ref[number]
        )
        for c in range(3):
            if entry[c] != 0:
                term = scalar * (entry[c] / LENGTHS[number])
                force[c] = term if force[c] is None else force[c] + term
    for c in range(3):
        v_new = v_ref[c] + TIME_STEP * (force[c] + load_ref[c])
        vnew_ref[c] = v_new
        unew_ref[c] = u_ref[c] + TIME_STEP * v_new


def compiler_params():
    return pltpu.CompilerParams(vmem_limit_bytes=100 * 1024 * 1024)


def local(displacement, velocity, bulk_modulus, shear_modulus, blast_load, loaded, broken):
    count = len(OFFSETS)
    cell_shape = displacement.shape[1:]
    cells_x, cells_y, cells_z = cell_shape
    index_x = lax.axis_index("gx")
    index_y = lax.axis_index("gy")
    index_z = lax.axis_index("gz")
    span_x = lax.axis_size("gx")
    span_y = lax.axis_size("gy")
    span_z = lax.axis_size("gz")
    along_x = {value: presence(cells_x, index_x, span_x, value) for value in range(-3, 4)}
    along_y = {value: presence(cells_y, index_y, span_y, value) for value in range(-3, 4)}
    along_z = {value: presence(cells_z, index_z, span_z, value) for value in range(-3, 4)}
    exists_x = jnp.stack([along_x[e[0]] for e in OFFSETS])
    exists_y = jnp.stack([along_y[e[1]] for e in OFFSETS])
    exists_z = jnp.stack([along_z[e[2]] for e in OFFSETS])
    exists = exists_x[:, :, None, None] * exists_y[:, None, :, None] * exists_z[:, None, None, :]
    squares = jnp.array([l * l for l in LENGTHS], jnp.float32)
    weight = jnp.sum(exists * squares[:, None, None, None], axis=0)
    shifts = jnp.arange(8, dtype=jnp.int32)
    bits = jnp.right_shift(broken[:, None], shifts[None, :, None, None, None]) & 1
    bits = bits.reshape((broken.shape[0] * 8,) + tuple(cell_shape))[:count]
    intact = exists * (1.0 - bits.astype(jnp.float32))
    stiffness = 15.0 * shear_modulus / weight
    load_force = loaded.astype(jnp.float32)[None] * blast_load
    modulus_factor = 3.0 * bulk_modulus - 5.0 * shear_modulus
    displacement_now = displacement
    velocity_now = velocity
    padded_stiffness = None
    f32 = jnp.float32
    pairs = len(PAIRS)
    halo_x = cells_x + 6

    def whole(shape):
        return pl.BlockSpec(shape, lambda block: (0,) * len(shape))

    bonds_spec = pl.BlockSpec((count, ROWS, cells_y, cells_z), lambda block: (0, block, 0, 0))
    cells_spec = pl.BlockSpec((ROWS, cells_y, cells_z), lambda block: (block, 0, 0))
    vector_spec = pl.BlockSpec((3, ROWS, cells_y, cells_z), lambda block: (0, block, 0, 0))
    for step_index in range(STEPS):
        if step_index == 0:
            extended = extend(jnp.concatenate([displacement_now, stiffness[None]], axis=0))
            padded_stiffness = extended[3]
        else:
            extended = extend(displacement_now)
        stretches, coupling = pl.pallas_call(
            stretch_kernel,
            out_shape=(
                jax.ShapeDtypeStruct((count,) + tuple(cell_shape), f32),
                jax.ShapeDtypeStruct(tuple(cell_shape), f32),
            ),
            grid=(cells_x // ROWS,),
            in_specs=[
                whole((3, halo_x, cells_y + 6, cells_z + 6)),
                bonds_spec,
                cells_spec,
                cells_spec,
            ],
            out_specs=(bonds_spec, cells_spec),
            scratch_shapes=[pltpu.VMEM((pairs, 3, halo_x, cells_y, cells_z), f32)],
            compiler_params=compiler_params(),
            interpret=INTERPRET,
        )(extended[:3], intact, weight, modulus_factor)
        padded_coupling = extended_2(coupling, (("gx", 0), ("gy", 1), ("gz", 2)), 3)
        displacement_now, velocity_now = pl.pallas_call(
            force_kernel,
            out_shape=(
                jax.ShapeDtypeStruct(displacement.shape, f32),
                jax.ShapeDtypeStruct(displacement.shape, f32),
            ),
            grid=(cells_x // ROWS,),
            in_specs=[
                whole((halo_x, cells_y + 6, cells_z + 6)),
                whole((halo_x, cells_y + 6, cells_z + 6)),
                bonds_spec,
                bonds_spec,
                vector_spec,
                vector_spec,
                vector_spec,
            ],
            out_specs=(vector_spec, vector_spec),
            scratch_shapes=[
                pltpu.VMEM((pairs, halo_x, cells_y, cells_z), f32),
                pltpu.VMEM((pairs, halo_x, cells_y, cells_z), f32),
            ],
            compiler_params=compiler_params(),
            interpret=INTERPRET,
        )(padded_coupling, padded_stiffness, stretches, intact, displacement_now, velocity_now, load_force)
    return (displacement_now, velocity_now)


def solution(mesh):
    placed = (
        P(None, "gx", "gy", "gz"),
        P(None, "gx", "gy", "gz"),
        P("gx", "gy", "gz"),
        P("gx", "gy", "gz"),
        P(None, "gx", "gy", "gz"),
        P("gx", "gy", "gz"),
        P(None, "gx", "gy", "gz"),
    )
    return jax.shard_map(
        local,
        mesh=mesh,
        in_specs=placed,
        out_specs=(P(None, "gx", "gy", "gz"), P(None, "gx", "gy", "gz")),
        check_vma=False,
    )
```

```python
import math

import jax
import jax.numpy as jnp
from jax import lax
from jax.experimental import pallas as pl
from jax.experimental.pallas import tpu as pltpu
from jax.sharding import PartitionSpec as P

STEPS = 2


TIME_STEP = 0.01

INTERPRET = False

ROWS = 4


def extended_2(cells, sides, width):
    for axis, dim in sides:
        count = lax.axis_size(axis)
        ends = count - 1
        head = lax.slice_in_dim(cells, 0, width, axis=dim)
        tail = lax.slice_in_dim(cells, cells.shape[dim] - width, cells.shape[dim], axis=dim)
        cells = jnp.concatenate(
            [
                lax.ppermute(tail.reshape(-1), axis, [(i, (i + 1) % count) for i in range(ends)]).reshape(tail.shape),
                cells,
                lax.ppermute(head.reshape(-1), axis, [((i + 1) % count, i) for i in range(ends)]).reshape(head.shape),
            ],
            axis=dim,
        )
    return cells


def offset_table():
    forward = []
    for step_x in range(-3, 4):
        for step_y in range(-3, 4):
            for step_z in range(-3, 4):
                squared = step_x * step_x + step_y * step_y + step_z * step_z
                if squared == 0 or squared > 9:
                    continue
                summed = step_x + step_y + step_z
                if summed > 0 or (summed == 0 and (step_x > 0 or (step_x == 0 and step_y > 0))):
                    forward.append((step_x, step_y, step_z))
    backward = []
    for entry in forward:
        backward.append((-entry[0], -entry[1], -entry[2]))
    return forward + backward


OFFSETS = offset_table()
LENGTHS = [math.sqrt(e[0] ** 2 + e[1] ** 2 + e[2] ** 2) for e in OFFSETS]
PAIRS = sorted({(e[1], e[2]) for e in OFFSETS} | {(0, 0)})
PAIR_OF = {pair: number for number, pair in enumerate(PAIRS)}


def presence(cell_count, device_index, device_count, offset_value):
    position = device_index * cell_count + jnp.arange(cell_count, dtype=jnp.int32) + offset_value
    return ((position >= 0) & (position < device_count * cell_count)).astype(jnp.float32)


def extend(values):
    return extended_2(values, (("gx", 1), ("gy", 2), ("gz", 3)), 3)


def fill_stack(stack_ref, padded_ref, leading, fills):
    cells_y, cells_z = stack_ref.shape[-2], stack_ref.shape[-1]
    for dst, src, rows in fills:
        for pair, (oy, oz) in enumerate(PAIRS):
            for c in leading:
                index = (pair, pl.ds(dst, rows)) if c is None else (pair, c, pl.ds(dst, rows))
                source = (pl.ds(src, rows),) if c is None else (c, pl.ds(src, rows))
                stack_ref[index] = padded_ref[source + (pl.ds(3 + oy, cells_y), pl.ds(3 + oz, cells_z))]


def stretch_kernel(first, stride, fills, aliased):
    def kernel(*refs):
        if aliased:
            ext_ref, intact_ref, weight_ref, factor_ref, _, _, stretch_ref, coupling_ref, us_ref = refs
        else:
            ext_ref, intact_ref, weight_ref, factor_ref, stretch_ref, coupling_ref, us_ref = refs
        step = pl.program_id(0)

        @pl.when(step == 0)
        def _():
            fill_stack(us_ref, ext_ref, (0, 1, 2), fills)

        centre = PAIR_OF[(0, 0)]
        x0 = pl.multiple_of((first + stride * step) * ROWS, ROWS)
        own = [us_ref[centre, c, pl.ds(x0 + 3, ROWS)] for c in range(3)]
        total = jnp.zeros_like(own[0])
        for number, entry in enumerate(OFFSETS):
            pair = PAIR_OF[(entry[1], entry[2])]
            squared = None
            for c in range(3):
                diff = us_ref[pair, c, pl.ds(x0 + 3 + entry[0], ROWS)] - own[c]
                if entry[c] != 0:
                    diff = diff + float(entry[c])
                squared = diff * diff if squared is None else squared + diff * diff
            value = jnp.sqrt(squared) - LENGTHS[number]
            stretch_ref[number] = value
            total = total + intact_ref[number] * LENGTHS[number] * value
        weight = weight_ref[...]
        dilatation = 3.0 * total / weight
        coupling_ref[...] = dilatation * factor_ref[...] / weight

    return kernel


def force_kernel(first, stride, fills, aliased):
    def kernel(*refs):
        if aliased:
            (pc_ref, ps_ref, stretch_ref, intact_ref, u_ref, v_ref, load_ref, _, _,
             unew_ref, vnew_ref, cs_ref, ss_ref) = refs
        else:
            (pc_ref, ps_ref, stretch_ref, intact_ref, u_ref, v_ref, load_ref,
             unew_ref, vnew_ref, cs_ref, ss_ref) = refs
        step = pl.program_id(0)

        @pl.when(step == 0)
        def _():
            fill_stack(cs_ref, pc_ref, (None,), fills)
            fill_stack(ss_ref, ps_ref, (None,), fills)

        centre = PAIR_OF[(0, 0)]
        x0 = pl.multiple_of((first + stride * step) * ROWS, ROWS)
        c_own = cs_ref[centre, pl.ds(x0 + 3, ROWS)]
        s_own = ss_ref[centre, pl.ds(x0 + 3, ROWS)]
        force = [None, None, None]
        for number, entry in enumerate(OFFSETS):
            pair = PAIR_OF[(entry[1], entry[2])]
            rows = pl.ds(x0 + 3 + entry[0], ROWS)
            scalar = intact_ref[number] * (
                LENGTHS[number] * (c_own + cs_ref[pair, rows])
                + (s_own + ss_ref[pair, rows]) * stretch_ref[number]
            )
            for c in range(3):
                if entry[c] != 0:
                    term = scalar * (entry[c] / LENGTHS[number])
                    force[c] = term if force[c] is None else force[c] + term
        for c in range(3):
            v_new = v_ref[c] + TIME_STEP * (force[c] + load_ref[c])
            vnew_ref[c] = v_new
            unew_ref[c] = u_ref[c] + TIME_STEP * v_new

    return kernel


def compiler_params():
    return pltpu.CompilerParams(vmem_limit_bytes=100 * 1024 * 1024)


def local(displacement, velocity, bulk_modulus, shear_modulus, blast_load, loaded, broken):
    count = len(OFFSETS)
    cell_shape = displacement.shape[1:]
    cells_x, cells_y, cells_z = cell_shape
    index_x = lax.axis_index("gx")
    index_y = lax.axis_index("gy")
    index_z = lax.axis_index("gz")
    span_x = lax.axis_size("gx")
    span_y = lax.axis_size("gy")
    span_z = lax.axis_size("gz")
    along_x = {value: presence(cells_x, index_x, span_x, value) for value in range(-3, 4)}
    along_y = {value: presence(cells_y, index_y, span_y, value) for value in range(-3, 4)}
    along_z = {value: presence(cells_z, index_z, span_z, value) for value in range(-3, 4)}
    exists_x = jnp.stack([along_x[e[0]] for e in OFFSETS])
    exists_y = jnp.stack([along_y[e[1]] for e in OFFSETS])
    exists_z = jnp.stack([along_z[e[2]] for e in OFFSETS])
    exists = exists_x[:, :, None, None] * exists_y[:, None, :, None] * exists_z[:, None, None, :]
    squares = jnp.array([l * l for l in LENGTHS], jnp.float32)
    weight = jnp.sum(exists * squares[:, None, None, None], axis=0)
    shifts = jnp.arange(8, dtype=jnp.int32)
    bits = jnp.right_shift(broken[:, None], shifts[None, :, None, None, None]) & 1
    bits = bits.reshape((broken.shape[0] * 8,) + tuple(cell_shape))[:count]
    intact = exists * (1.0 - bits.astype(jnp.float32))
    stiffness = 15.0 * shear_modulus / weight
    load_force = loaded.astype(jnp.float32)[None] * blast_load
    modulus_factor = 3.0 * bulk_modulus - 5.0 * shear_modulus
    displacement_now = displacement
    velocity_now = velocity
    f32 = jnp.float32
    pairs = len(PAIRS)
    halo_x = cells_x + 6
    blocks = cells_x // ROWS
    middle_count = blocks - 2
    any_spec = pl.BlockSpec(memory_space=pl.ANY)
    middle_fill = ((ROWS, ROWS - 3, cells_x - 2 * ROWS + 6),)
    edge_fill = ((0, 0, ROWS + 6), (halo_x - ROWS - 6, halo_x - ROWS - 6, ROWS + 6))

    def whole(shape):
        return pl.BlockSpec(shape, lambda step: (0,) * len(shape))

    def specs(first, stride):
        return (
            pl.BlockSpec((count, ROWS, cells_y, cells_z), lambda step: (0, first + stride * step, 0, 0)),
            pl.BlockSpec((ROWS, cells_y, cells_z), lambda step: (first + stride * step, 0, 0)),
            pl.BlockSpec((3, ROWS, cells_y, cells_z), lambda step: (0, first + stride * step, 0, 0)),
        )

    yz_sides = (("gy", 2), ("gz", 3))
    x_side = (("gx", 1),)
    yz_stiffness = None
    padded_stiffness = None
    for step_index in range(STEPS):
        if step_index == 0:
            yz = extended_2(jnp.concatenate([displacement_now, stiffness[None]], axis=0), yz_sides, 3)
            extended = extended_2(yz, x_side, 3)
            yz_stiffness = yz[3]
            padded_stiffness = extended[3]
            yz = yz[:3]
            extended = extended[:3]
        else:
            yz = extended_2(displacement_now, yz_sides, 3)
            extended = extended_2(yz, x_side, 3)
        bonds_m, cells_m, vector_m = specs(1, 1)
        bonds_e, cells_e, vector_e = specs(0, blocks - 1)
        stretch_shapes = (
            jax.ShapeDtypeStruct((count,) + tuple(cell_shape), f32),
            jax.ShapeDtypeStruct(tuple(cell_shape), f32),
        )
        stretches, coupling = pl.pallas_call(
            stretch_kernel(1, 1, middle_fill, False),
            out_shape=stretch_shapes,
            grid=(middle_count,),
            in_specs=[whole((3, cells_x, cells_y + 6, cells_z + 6)), bonds_m, cells_m, cells_m],
            out_specs=(bonds_m, cells_m),
            scratch_shapes=[pltpu.VMEM((pairs, 3, halo_x, cells_y, cells_z), f32)],
            compiler_params=compiler_params(),
            interpret=INTERPRET,
        )(yz, intact, weight, modulus_factor)
        stretches, coupling = pl.pallas_call(
            stretch_kernel(0, blocks - 1, edge_fill, True),
            out_shape=stretch_shapes,
            grid=(2,),
            in_specs=[whole((3, halo_x, cells_y + 6, cells_z + 6)), bonds_e, cells_e, cells_e, any_spec, any_spec],
            out_specs=(bonds_e, cells_e),
            scratch_shapes=[pltpu.VMEM((pairs, 3, halo_x, cells_y, cells_z), f32)],
            input_output_aliases={4: 0, 5: 1},
            compiler_params=compiler_params(),
            interpret=INTERPRET,
        )(extended, intact, weight, modulus_factor, stretches, coupling)
        yz_coupling = extended_2(coupling, (("gy", 1), ("gz", 2)), 3)
        padded_coupling = extended_2(yz_coupling, (("gx", 0),), 3)
        vector_shapes = (
            jax.ShapeDtypeStruct(displacement.shape, f32),
            jax.ShapeDtypeStruct(displacement.shape, f32),
        )
        force_scratch = [
            pltpu.VMEM((pairs, halo_x, cells_y, cells_z), f32),
            pltpu.VMEM((pairs, halo_x, cells_y, cells_z), f32),
        ]
        new_u, new_v = pl.pallas_call(
            force_kernel(1, 1, middle_fill, False),
            out_shape=vector_shapes,
            grid=(middle_count,),
            in_specs=[
                whole((cells_x, cells_y + 6, cells_z + 6)),
                whole((cells_x, cells_y + 6, cells_z + 6)),
                bonds_m, bonds_m, vector_m, vector_m, vector_m,
            ],
            out_specs=(vector_m, vector_m),
            scratch_shapes=force_scratch,
            compiler_params=compiler_params(),
            interpret=INTERPRET,
        )(yz_coupling, yz_stiffness, stretches, intact, displacement_now, velocity_now, load_force)
        displacement_now, velocity_now = pl.pallas_call(
            force_kernel(0, blocks - 1, edge_fill, True),
            out_shape=vector_shapes,
            grid=(2,),
            in_specs=[
                whole((halo_x, cells_y + 6, cells_z + 6)),
                whole((halo_x, cells_y + 6, cells_z + 6)),
                bonds_e, bonds_e, vector_e, vector_e, vector_e, any_spec, any_spec,
            ],
            out_specs=(vector_e, vector_e),
            scratch_shapes=force_scratch,
            input_output_aliases={7: 0, 8: 1},
            compiler_params=compiler_params(),
            interpret=INTERPRET,
        )(padded_coupling, padded_stiffness, stretches, intact, displacement_now, velocity_now, load_force, new_u, new_v)
    return (displacement_now, velocity_now)


def solution(mesh):
    placed = (
        P(None, "gx", "gy", "gz"),
        P(None, "gx", "gy", "gz"),
        P("gx", "gy", "gz"),
        P("gx", "gy", "gz"),
        P(None, "gx", "gy", "gz"),
        P("gx", "gy", "gz"),
        P(None, "gx", "gy", "gz"),
    )
    return jax.shard_map(
        local,
        mesh=mesh,
        in_specs=placed,
        out_specs=(P(None, "gx", "gy", "gz"), P(None, "gx", "gy", "gz")),
        check_vma=False,
    )
```

```python
import math

import jax
import jax.numpy as jnp
from jax import lax
from jax.experimental import pallas as pl
from jax.experimental.pallas import tpu as pltpu
from jax.sharding import PartitionSpec as P

STEPS = 2


TIME_STEP = 0.01

INTERPRET = False

ROWS = 4


def extended_2(cells, sides, width):
    for axis, dim in sides:
        count = lax.axis_size(axis)
        ends = count - 1
        head = lax.slice_in_dim(cells, 0, width, axis=dim)
        tail = lax.slice_in_dim(cells, cells.shape[dim] - width, cells.shape[dim], axis=dim)
        cells = jnp.concatenate(
            [
                lax.ppermute(tail.reshape(-1), axis, [(i, (i + 1) % count) for i in range(ends)]).reshape(tail.shape),
                cells,
                lax.ppermute(head.reshape(-1), axis, [((i + 1) % count, i) for i in range(ends)]).reshape(head.shape),
            ],
            axis=dim,
        )
    return cells


def offset_table():
    forward = []
    for step_x in range(-3, 4):
        for step_y in range(-3, 4):
            for step_z in range(-3, 4):
                squared = step_x * step_x + step_y * step_y + step_z * step_z
                if squared == 0 or squared > 9:
                    continue
                summed = step_x + step_y + step_z
                if summed > 0 or (summed == 0 and (step_x > 0 or (step_x == 0 and step_y > 0))):
                    forward.append((step_x, step_y, step_z))
    backward = []
    for entry in forward:
        backward.append((-entry[0], -entry[1], -entry[2]))
    return forward + backward


OFFSETS = offset_table()
LENGTHS = [math.sqrt(e[0] ** 2 + e[1] ** 2 + e[2] ** 2) for e in OFFSETS]
PAIRS = sorted({(e[1], e[2]) for e in OFFSETS} | {(0, 0)})
PAIR_OF = {pair: number for number, pair in enumerate(PAIRS)}


def presence(cell_count, device_index, device_count, offset_value):
    position = device_index * cell_count + jnp.arange(cell_count, dtype=jnp.int32) + offset_value
    return ((position >= 0) & (position < device_count * cell_count)).astype(jnp.float32)


def extend(values):
    return extended_2(values, (("gx", 1), ("gy", 2), ("gz", 3)), 3)


def fill_stack(stack_ref, padded_ref, leading):
    cells_y, cells_z = stack_ref.shape[-2], stack_ref.shape[-1]

    def row(index, carry):
        for pair, (oy, oz) in enumerate(PAIRS):
            for c in leading:
                target = (pair, pl.ds(index, 1)) if c is None else (pair, c, pl.ds(index, 1))
                source = (pl.ds(index, 1),) if c is None else (c, pl.ds(index, 1))
                stack_ref[target] = padded_ref[source + (pl.ds(3 + oy, cells_y), pl.ds(3 + oz, cells_z))]
        return carry

    lax.fori_loop(0, stack_ref.shape[-3], row, 0)


def stretch_kernel(ext_ref, intact_ref, weight_ref, factor_ref, stretch_ref, coupling_ref, us_ref):
    block = pl.program_id(0)

    @pl.when(block == 0)
    def _():
        fill_stack(us_ref, ext_ref, (0, 1, 2))

    centre = PAIR_OF[(0, 0)]
    x0 = pl.multiple_of(block * ROWS, ROWS)
    own = [us_ref[centre, c, pl.ds(x0 + 3, ROWS)] for c in range(3)]
    total = jnp.zeros_like(own[0])
    for number, entry in enumerate(OFFSETS):
        pair = PAIR_OF[(entry[1], entry[2])]
        squared = None
        for c in range(3):
            diff = us_ref[pair, c, pl.ds(x0 + 3 + entry[0], ROWS)] - own[c]
            if entry[c] != 0:
                diff = diff + float(entry[c])
            squared = diff * diff if squared is None else squared + diff * diff
        value = jnp.sqrt(squared) - LENGTHS[number]
        stretch_ref[number] = value
        total = total + intact_ref[number] * LENGTHS[number] * value
    weight = weight_ref[...]
    dilatation = 3.0 * total / weight
    coupling_ref[...] = dilatation * factor_ref[...] / weight


def force_kernel(pc_ref, ps_ref, stretch_ref, intact_ref, u_ref, v_ref, load_ref, unew_ref, vnew_ref, cs_ref, ss_ref):
    block = pl.program_id(0)

    @pl.when(block == 0)
    def _():
        fill_stack(cs_ref, pc_ref, (None,))
        fill_stack(ss_ref, ps_ref, (None,))

    centre = PAIR_OF[(0, 0)]
    x0 = pl.multiple_of(block * ROWS, ROWS)
    c_own = cs_ref[centre, pl.ds(x0 + 3, ROWS)]
    s_own = ss_ref[centre, pl.ds(x0 + 3, ROWS)]
    force = [None, None, None]
    for number, entry in enumerate(OFFSETS):
        pair = PAIR_OF[(entry[1], entry[2])]
        rows = pl.ds(x0 + 3 + entry[0], ROWS)
        scalar = intact_ref[number] * (
            LENGTHS[number] * (c_own + cs_ref[pair, rows])
            + (s_own + ss_ref[pair, rows]) * stretch_ref[number]
        )
        for c in range(3):
            if entry[c] != 0:
                term = scalar * (entry[c] / LENGTHS[number])
                force[c] = term if force[c] is None else force[c] + term
    for c in range(3):
        v_new = v_ref[c] + TIME_STEP * (force[c] + load_ref[c])
        vnew_ref[c] = v_new
        unew_ref[c] = u_ref[c] + TIME_STEP * v_new


def compiler_params():
    return pltpu.CompilerParams(vmem_limit_bytes=100 * 1024 * 1024)


def local(displacement, velocity, bulk_modulus, shear_modulus, blast_load, loaded, broken):
    count = len(OFFSETS)
    cell_shape = displacement.shape[1:]
    cells_x, cells_y, cells_z = cell_shape
    index_x = lax.axis_index("gx")
    index_y = lax.axis_index("gy")
    index_z = lax.axis_index("gz")
    span_x = lax.axis_size("gx")
    span_y = lax.axis_size("gy")
    span_z = lax.axis_size("gz")
    along_x = {value: presence(cells_x, index_x, span_x, value) for value in range(-3, 4)}
    along_y = {value: presence(cells_y, index_y, span_y, value) for value in range(-3, 4)}
    along_z = {value: presence(cells_z, index_z, span_z, value) for value in range(-3, 4)}
    exists_x = jnp.stack([along_x[e[0]] for e in OFFSETS])
    exists_y = jnp.stack([along_y[e[1]] for e in OFFSETS])
    exists_z = jnp.stack([along_z[e[2]] for e in OFFSETS])
    exists = exists_x[:, :, None, None] * exists_y[:, None, :, None] * exists_z[:, None, None, :]
    squares = jnp.array([l * l for l in LENGTHS], jnp.float32)
    weight = jnp.sum(exists * squares[:, None, None, None], axis=0)
    shifts = jnp.arange(8, dtype=jnp.int32)
    bits = jnp.right_shift(broken[:, None], shifts[None, :, None, None, None]) & 1
    bits = bits.reshape((broken.shape[0] * 8,) + tuple(cell_shape))[:count]
    intact = exists * (1.0 - bits.astype(jnp.float32))
    stiffness = 15.0 * shear_modulus / weight
    load_force = loaded.astype(jnp.float32)[None] * blast_load
    modulus_factor = 3.0 * bulk_modulus - 5.0 * shear_modulus
    displacement_now = displacement
    velocity_now = velocity
    padded_stiffness = None
    f32 = jnp.float32
    pairs = len(PAIRS)
    halo_x = cells_x + 6

    def whole(shape):
        return pl.BlockSpec(shape, lambda block: (0,) * len(shape))

    bonds_spec = pl.BlockSpec((count, ROWS, cells_y, cells_z), lambda block: (0, block, 0, 0))
    cells_spec = pl.BlockSpec((ROWS, cells_y, cells_z), lambda block: (block, 0, 0))
    vector_spec = pl.BlockSpec((3, ROWS, cells_y, cells_z), lambda block: (0, block, 0, 0))
    for step_index in range(STEPS):
        if step_index == 0:
            extended = extend(jnp.concatenate([displacement_now, stiffness[None]], axis=0))
            padded_stiffness = extended[3]
        else:
            extended = extend(displacement_now)
        stretches, coupling = pl.pallas_call(
            stretch_kernel,
            out_shape=(
                jax.ShapeDtypeStruct((count,) + tuple(cell_shape), f32),
                jax.ShapeDtypeStruct(tuple(cell_shape), f32),
            ),
            grid=(cells_x // ROWS,),
            in_specs=[
                whole((3, halo_x, cells_y + 6, cells_z + 6)),
                bonds_spec,
                cells_spec,
                cells_spec,
            ],
            out_specs=(bonds_spec, cells_spec),
            scratch_shapes=[pltpu.VMEM((pairs, 3, halo_x, cells_y, cells_z), f32)],
            compiler_params=compiler_params(),
            interpret=INTERPRET,
        )(extended[:3], intact, weight, modulus_factor)
        padded_coupling = extended_2(coupling, (("gx", 0), ("gy", 1), ("gz", 2)), 3)
        displacement_now, velocity_now = pl.pallas_call(
            force_kernel,
            out_shape=(
                jax.ShapeDtypeStruct(displacement.shape, f32),
                jax.ShapeDtypeStruct(displacement.shape, f32),
            ),
            grid=(cells_x // ROWS,),
            in_specs=[
                whole((halo_x, cells_y + 6, cells_z + 6)),
                whole((halo_x, cells_y + 6, cells_z + 6)),
                bonds_spec,
                bonds_spec,
                vector_spec,
                vector_spec,
                vector_spec,
            ],
            out_specs=(vector_spec, vector_spec),
            scratch_shapes=[
                pltpu.VMEM((pairs, halo_x, cells_y, cells_z), f32),
                pltpu.VMEM((pairs, halo_x, cells_y, cells_z), f32),
            ],
            compiler_params=compiler_params(),
            interpret=INTERPRET,
        )(padded_coupling, padded_stiffness, stretches, intact, displacement_now, velocity_now, load_force)
    return (displacement_now, velocity_now)


def solution(mesh):
    placed = (
        P(None, "gx", "gy", "gz"),
        P(None, "gx", "gy", "gz"),
        P("gx", "gy", "gz"),
        P("gx", "gy", "gz"),
        P(None, "gx", "gy", "gz"),
        P("gx", "gy", "gz"),
        P(None, "gx", "gy", "gz"),
    )
    return jax.shard_map(
        local,
        mesh=mesh,
        in_specs=placed,
        out_specs=(P(None, "gx", "gy", "gz"), P(None, "gx", "gy", "gz")),
        check_vma=False,
    )
```

```python
import math

import jax
import jax.numpy as jnp
from jax import lax
from jax.experimental import pallas as pl
from jax.experimental.pallas import tpu as pltpu
from jax.sharding import PartitionSpec as P

STEPS = 2


TIME_STEP = 0.01

INTERPRET = False

ROWS = 4


def extended_2(cells, sides, width):
    for axis, dim in sides:
        count = lax.axis_size(axis)
        ends = count - 1
        head = lax.slice_in_dim(cells, 0, width, axis=dim)
        tail = lax.slice_in_dim(cells, cells.shape[dim] - width, cells.shape[dim], axis=dim)
        cells = jnp.concatenate(
            [
                lax.ppermute(tail.reshape(-1), axis, [(i, (i + 1) % count) for i in range(ends)]).reshape(tail.shape),
                cells,
                lax.ppermute(head.reshape(-1), axis, [((i + 1) % count, i) for i in range(ends)]).reshape(head.shape),
            ],
            axis=dim,
        )
    return cells


def offset_table():
    forward = []
    for step_x in range(-3, 4):
        for step_y in range(-3, 4):
            for step_z in range(-3, 4):
                squared = step_x * step_x + step_y * step_y + step_z * step_z
                if squared == 0 or squared > 9:
                    continue
                summed = step_x + step_y + step_z
                if summed > 0 or (summed == 0 and (step_x > 0 or (step_x == 0 and step_y > 0))):
                    forward.append((step_x, step_y, step_z))
    backward = []
    for entry in forward:
        backward.append((-entry[0], -entry[1], -entry[2]))
    return forward + backward


OFFSETS = offset_table()
LENGTHS = [math.sqrt(e[0] ** 2 + e[1] ** 2 + e[2] ** 2) for e in OFFSETS]
PAIRS = sorted({(e[1], e[2]) for e in OFFSETS} | {(0, 0)})
PAIR_OF = {pair: number for number, pair in enumerate(PAIRS)}


def presence(cell_count, device_index, device_count, offset_value):
    position = device_index * cell_count + jnp.arange(cell_count, dtype=jnp.int32) + offset_value
    return ((position >= 0) & (position < device_count * cell_count)).astype(jnp.float32)


def extend(values):
    return extended_2(values, (("gx", 1), ("gy", 2), ("gz", 3)), 3)


def fill_stack(stack_ref, padded_ref, leading):
    cells_y, cells_z = stack_ref.shape[-2], stack_ref.shape[-1]
    trips = 2
    chunk = stack_ref.shape[-3] // trips

    def rows(trip, carry):
        start = trip * chunk
        for pair, (oy, oz) in enumerate(PAIRS):
            for c in leading:
                target = (pair, pl.ds(start, chunk)) if c is None else (pair, c, pl.ds(start, chunk))
                source = (pl.ds(start, chunk),) if c is None else (c, pl.ds(start, chunk))
                stack_ref[target] = padded_ref[source + (pl.ds(3 + oy, cells_y), pl.ds(3 + oz, cells_z))]
        return carry

    lax.fori_loop(0, trips, rows, 0)


def stretch_kernel(ext_ref, intact_ref, weight_ref, factor_ref, stretch_ref, coupling_ref, us_ref):
    block = pl.program_id(0)

    @pl.when(block == 0)
    def _():
        fill_stack(us_ref, ext_ref, (0, 1, 2))

    centre = PAIR_OF[(0, 0)]
    x0 = pl.multiple_of(block * ROWS, ROWS)
    own = [us_ref[centre, c, pl.ds(x0 + 3, ROWS)] for c in range(3)]
    total = jnp.zeros_like(own[0])
    for number, entry in enumerate(OFFSETS):
        pair = PAIR_OF[(entry[1], entry[2])]
        squared = None
        for c in range(3):
            diff = us_ref[pair, c, pl.ds(x0 + 3 + entry[0], ROWS)] - own[c]
            if entry[c] != 0:
                diff = diff + float(entry[c])
            squared = diff * diff if squared is None else squared + diff * diff
        value = jnp.sqrt(squared) - LENGTHS[number]
        stretch_ref[number] = value
        total = total + intact_ref[number] * LENGTHS[number] * value
    weight = weight_ref[...]
    dilatation = 3.0 * total / weight
    coupling_ref[...] = dilatation * factor_ref[...] / weight


def force_kernel(pc_ref, ps_ref, stretch_ref, intact_ref, u_ref, v_ref, load_ref, unew_ref, vnew_ref, cs_ref, ss_ref):
    block = pl.program_id(0)

    @pl.when(block == 0)
    def _():
        fill_stack(cs_ref, pc_ref, (None,))
        fill_stack(ss_ref, ps_ref, (None,))

    centre = PAIR_OF[(0, 0)]
    x0 = pl.multiple_of(block * ROWS, ROWS)
    c_own = cs_ref[centre, pl.ds(x0 + 3, ROWS)]
    s_own = ss_ref[centre, pl.ds(x0 + 3, ROWS)]
    force = [None, None, None]
    for number, entry in enumerate(OFFSETS):
        pair = PAIR_OF[(entry[1], entry[2])]
        rows = pl.ds(x0 + 3 + entry[0], ROWS)
        scalar = intact_ref[number] * (
            LENGTHS[number] * (c_own + cs_ref[pair, rows])
            + (s_own + ss_ref[pair, rows]) * stretch_ref[number]
        )
        for c in range(3):
            if entry[c] != 0:
                term = scalar * (entry[c] / LENGTHS[number])
                force[c] = term if force[c] is None else force[c] + term
    for c in range(3):
        v_new = v_ref[c] + TIME_STEP * (force[c] + load_ref[c])
        vnew_ref[c] = v_new
        unew_ref[c] = u_ref[c] + TIME_STEP * v_new


def compiler_params():
    return pltpu.CompilerParams(vmem_limit_bytes=100 * 1024 * 1024)


def local(displacement, velocity, bulk_modulus, shear_modulus, blast_load, loaded, broken):
    count = len(OFFSETS)
    cell_shape = displacement.shape[1:]
    cells_x, cells_y, cells_z = cell_shape
    index_x = lax.axis_index("gx")
    index_y = lax.axis_index("gy")
    index_z = lax.axis_index("gz")
    span_x = lax.axis_size("gx")
    span_y = lax.axis_size("gy")
    span_z = lax.axis_size("gz")
    along_x = {value: presence(cells_x, index_x, span_x, value) for value in range(-3, 4)}
    along_y = {value: presence(cells_y, index_y, span_y, value) for value in range(-3, 4)}
    along_z = {value: presence(cells_z, index_z, span_z, value) for value in range(-3, 4)}
    exists_x = jnp.stack([along_x[e[0]] for e in OFFSETS])
    exists_y = jnp.stack([along_y[e[1]] for e in OFFSETS])
    exists_z = jnp.stack([along_z[e[2]] for e in OFFSETS])
    exists = exists_x[:, :, None, None] * exists_y[:, None, :, None] * exists_z[:, None, None, :]
    squares = jnp.array([l * l for l in LENGTHS], jnp.float32)
    weight = jnp.sum(exists * squares[:, None, None, None], axis=0)
    shifts = jnp.arange(8, dtype=jnp.int32)
    bits = jnp.right_shift(broken[:, None], shifts[None, :, None, None, None]) & 1
    bits = bits.reshape((broken.shape[0] * 8,) + tuple(cell_shape))[:count]
    intact = exists * (1.0 - bits.astype(jnp.float32))
    stiffness = 15.0 * shear_modulus / weight
    load_force = loaded.astype(jnp.float32)[None] * blast_load
    modulus_factor = 3.0 * bulk_modulus - 5.0 * shear_modulus
    displacement_now = displacement
    velocity_now = velocity
    padded_stiffness = None
    f32 = jnp.float32
    pairs = len(PAIRS)
    halo_x = cells_x + 6

    def whole(shape):
        return pl.BlockSpec(shape, lambda block: (0,) * len(shape))

    bonds_spec = pl.BlockSpec((count, ROWS, cells_y, cells_z), lambda block: (0, block, 0, 0))
    cells_spec = pl.BlockSpec((ROWS, cells_y, cells_z), lambda block: (block, 0, 0))
    vector_spec = pl.BlockSpec((3, ROWS, cells_y, cells_z), lambda block: (0, block, 0, 0))
    for step_index in range(STEPS):
        if step_index == 0:
            extended = extend(jnp.concatenate([displacement_now, stiffness[None]], axis=0))
            padded_stiffness = extended[3]
        else:
            extended = extend(displacement_now)
        stretches, coupling = pl.pallas_call(
            stretch_kernel,
            out_shape=(
                jax.ShapeDtypeStruct((count,) + tuple(cell_shape), f32),
                jax.ShapeDtypeStruct(tuple(cell_shape), f32),
            ),
            grid=(cells_x // ROWS,),
            in_specs=[
                whole((3, halo_x, cells_y + 6, cells_z + 6)),
                bonds_spec,
                cells_spec,
                cells_spec,
            ],
            out_specs=(bonds_spec, cells_spec),
            scratch_shapes=[pltpu.VMEM((pairs, 3, halo_x, cells_y, cells_z), f32)],
            compiler_params=compiler_params(),
            interpret=INTERPRET,
        )(extended[:3], intact, weight, modulus_factor)
        padded_coupling = extended_2(coupling, (("gx", 0), ("gy", 1), ("gz", 2)), 3)
        displacement_now, velocity_now = pl.pallas_call(
            force_kernel,
            out_shape=(
                jax.ShapeDtypeStruct(displacement.shape, f32),
                jax.ShapeDtypeStruct(displacement.shape, f32),
            ),
            grid=(cells_x // ROWS,),
            in_specs=[
                whole((halo_x, cells_y + 6, cells_z + 6)),
                whole((halo_x, cells_y + 6, cells_z + 6)),
                bonds_spec,
                bonds_spec,
                vector_spec,
                vector_spec,
                vector_spec,
            ],
            out_specs=(vector_spec, vector_spec),
            scratch_shapes=[
                pltpu.VMEM((pairs, halo_x, cells_y, cells_z), f32),
                pltpu.VMEM((pairs, halo_x, cells_y, cells_z), f32),
            ],
            compiler_params=compiler_params(),
            interpret=INTERPRET,
        )(padded_coupling, padded_stiffness, stretches, intact, displacement_now, velocity_now, load_force)
    return (displacement_now, velocity_now)


def solution(mesh):
    placed = (
        P(None, "gx", "gy", "gz"),
        P(None, "gx", "gy", "gz"),
        P("gx", "gy", "gz"),
        P("gx", "gy", "gz"),
        P(None, "gx", "gy", "gz"),
        P("gx", "gy", "gz"),
        P(None, "gx", "gy", "gz"),
    )
    return jax.shard_map(
        local,
        mesh=mesh,
        in_specs=placed,
        out_specs=(P(None, "gx", "gy", "gz"), P(None, "gx", "gy", "gz")),
        check_vma=False,
    )
```

```python
import math

import jax
import jax.numpy as jnp
from jax import lax
from jax.experimental import pallas as pl
from jax.experimental.pallas import tpu as pltpu
from jax.sharding import PartitionSpec as P

STEPS = 2


TIME_STEP = 0.01

INTERPRET = False

ROWS = 4


def extended_2(cells, sides, width):
    for axis, dim in sides:
        count = lax.axis_size(axis)
        ends = count - 1
        head = lax.slice_in_dim(cells, 0, width, axis=dim)
        tail = lax.slice_in_dim(cells, cells.shape[dim] - width, cells.shape[dim], axis=dim)
        cells = jnp.concatenate(
            [
                lax.ppermute(tail.reshape(-1), axis, [(i, (i + 1) % count) for i in range(ends)]).reshape(tail.shape),
                cells,
                lax.ppermute(head.reshape(-1), axis, [((i + 1) % count, i) for i in range(ends)]).reshape(head.shape),
            ],
            axis=dim,
        )
    return cells


def offset_table():
    forward = []
    for step_x in range(-3, 4):
        for step_y in range(-3, 4):
            for step_z in range(-3, 4):
                squared = step_x * step_x + step_y * step_y + step_z * step_z
                if squared == 0 or squared > 9:
                    continue
                summed = step_x + step_y + step_z
                if summed > 0 or (summed == 0 and (step_x > 0 or (step_x == 0 and step_y > 0))):
                    forward.append((step_x, step_y, step_z))
    backward = []
    for entry in forward:
        backward.append((-entry[0], -entry[1], -entry[2]))
    return forward + backward


OFFSETS = offset_table()
LENGTHS = [math.sqrt(e[0] ** 2 + e[1] ** 2 + e[2] ** 2) for e in OFFSETS]
PAIRS = sorted({(e[1], e[2]) for e in OFFSETS} | {(0, 0)})
PAIR_OF = {pair: number for number, pair in enumerate(PAIRS)}


def presence(cell_count, device_index, device_count, offset_value):
    position = device_index * cell_count + jnp.arange(cell_count, dtype=jnp.int32) + offset_value
    return ((position >= 0) & (position < device_count * cell_count)).astype(jnp.float32)


def extend(values):
    return extended_2(values, (("gx", 1), ("gy", 2), ("gz", 3)), 3)


def fill_stack(stack_ref, padded_ref, leading):
    cells_y, cells_z = stack_ref.shape[-2], stack_ref.shape[-1]
    trips = 2
    chunk = stack_ref.shape[-3] // trips

    def rows(trip, carry):
        start = trip * chunk
        for pair, (oy, oz) in enumerate(PAIRS):
            for c in leading:
                target = (pair, pl.ds(start, chunk)) if c is None else (pair, c, pl.ds(start, chunk))
                source = (pl.ds(start, chunk),) if c is None else (c, pl.ds(start, chunk))
                stack_ref[target] = padded_ref[source + (pl.ds(3 + oy, cells_y), pl.ds(3 + oz, cells_z))]
        return carry

    lax.fori_loop(0, trips, rows, 0)


def stretch_kernel(ext_ref, intact_ref, weight_ref, factor_ref, stretch_ref, coupling_ref, us_ref):
    block = pl.program_id(0)

    @pl.when(block == 0)
    def _():
        fill_stack(us_ref, ext_ref, (0, 1, 2))

    centre = PAIR_OF[(0, 0)]
    x0 = pl.multiple_of(block * ROWS, ROWS)
    own = [us_ref[centre, c, pl.ds(x0 + 3, ROWS)] for c in range(3)]
    total = jnp.zeros_like(own[0])
    for number, entry in enumerate(OFFSETS):
        pair = PAIR_OF[(entry[1], entry[2])]
        squared = None
        for c in range(3):
            diff = us_ref[pair, c, pl.ds(x0 + 3 + entry[0], ROWS)] - own[c]
            if entry[c] != 0:
                diff = diff + float(entry[c])
            squared = diff * diff if squared is None else squared + diff * diff
        value = jnp.sqrt(squared) - LENGTHS[number]
        stretch_ref[number] = value
        total = total + intact_ref[number] * LENGTHS[number] * value
    weight = weight_ref[...]
    dilatation = 3.0 * total / weight
    coupling_ref[...] = dilatation * factor_ref[...] / weight


def force_kernel(pc_ref, ps_ref, stretch_ref, intact_ref, u_ref, v_ref, load_ref, unew_ref, vnew_ref, cs_ref, ss_ref):
    block = pl.program_id(0)

    @pl.when(block == 0)
    def _():
        fill_stack(cs_ref, pc_ref, (None,))
        fill_stack(ss_ref, ps_ref, (None,))

    centre = PAIR_OF[(0, 0)]
    x0 = pl.multiple_of(block * ROWS, ROWS)
    c_own = cs_ref[centre, pl.ds(x0 + 3, ROWS)]
    s_own = ss_ref[centre, pl.ds(x0 + 3, ROWS)]
    force = [None, None, None]
    for number, entry in enumerate(OFFSETS):
        pair = PAIR_OF[(entry[1], entry[2])]
        rows = pl.ds(x0 + 3 + entry[0], ROWS)
        scalar = intact_ref[number] * (
            LENGTHS[number] * (c_own + cs_ref[pair, rows])
            + (s_own + ss_ref[pair, rows]) * stretch_ref[number]
        )
        for c in range(3):
            if entry[c] != 0:
                term = scalar * (entry[c] / LENGTHS[number])
                force[c] = term if force[c] is None else force[c] + term
    for c in range(3):
        v_new = v_ref[c] + TIME_STEP * (force[c] + load_ref[c])
        vnew_ref[c] = v_new
        unew_ref[c] = u_ref[c] + TIME_STEP * v_new


def compiler_params():
    return pltpu.CompilerParams(vmem_limit_bytes=100 * 1024 * 1024)


def local(displacement, velocity, bulk_modulus, shear_modulus, blast_load, loaded, broken):
    count = len(OFFSETS)
    cell_shape = displacement.shape[1:]
    cells_x, cells_y, cells_z = cell_shape
    index_x = lax.axis_index("gx")
    index_y = lax.axis_index("gy")
    index_z = lax.axis_index("gz")
    span_x = lax.axis_size("gx")
    span_y = lax.axis_size("gy")
    span_z = lax.axis_size("gz")
    along_x = {value: presence(cells_x, index_x, span_x, value) for value in range(-3, 4)}
    along_y = {value: presence(cells_y, index_y, span_y, value) for value in range(-3, 4)}
    along_z = {value: presence(cells_z, index_z, span_z, value) for value in range(-3, 4)}
    exists_x = jnp.stack([along_x[e[0]] for e in OFFSETS])
    exists_y = jnp.stack([along_y[e[1]] for e in OFFSETS])
    exists_z = jnp.stack([along_z[e[2]] for e in OFFSETS])
    exists = exists_x[:, :, None, None] * exists_y[:, None, :, None] * exists_z[:, None, None, :]
    squares = jnp.array([l * l for l in LENGTHS], jnp.float32)
    weight = jnp.sum(exists * squares[:, None, None, None], axis=0)
    shifts = jnp.array([number % 8 for number in range(count)], jnp.int32)[:, None, None, None]
    words = jnp.repeat(broken, 8, axis=0)[:count]
    bits = jnp.right_shift(words, shifts) & 1
    intact = exists * (1.0 - bits.astype(jnp.float32))
    stiffness = 15.0 * shear_modulus / weight
    load_force = loaded.astype(jnp.float32)[None] * blast_load
    modulus_factor = 3.0 * bulk_modulus - 5.0 * shear_modulus
    displacement_now = displacement
    velocity_now = velocity
    padded_stiffness = None
    f32 = jnp.float32
    pairs = len(PAIRS)
    halo_x = cells_x + 6

    def whole(shape):
        return pl.BlockSpec(shape, lambda block: (0,) * len(shape))

    bonds_spec = pl.BlockSpec((count, ROWS, cells_y, cells_z), lambda block: (0, block, 0, 0))
    cells_spec = pl.BlockSpec((ROWS, cells_y, cells_z), lambda block: (block, 0, 0))
    vector_spec = pl.BlockSpec((3, ROWS, cells_y, cells_z), lambda block: (0, block, 0, 0))
    for step_index in range(STEPS):
        if step_index == 0:
            extended = extend(jnp.concatenate([displacement_now, stiffness[None]], axis=0))
            padded_stiffness = extended[3]
        else:
            extended = extend(displacement_now)
        stretches, coupling = pl.pallas_call(
            stretch_kernel,
            out_shape=(
                jax.ShapeDtypeStruct((count,) + tuple(cell_shape), f32),
                jax.ShapeDtypeStruct(tuple(cell_shape), f32),
            ),
            grid=(cells_x // ROWS,),
            in_specs=[
                whole((3, halo_x, cells_y + 6, cells_z + 6)),
                bonds_spec,
                cells_spec,
                cells_spec,
            ],
            out_specs=(bonds_spec, cells_spec),
            scratch_shapes=[pltpu.VMEM((pairs, 3, halo_x, cells_y, cells_z), f32)],
            compiler_params=compiler_params(),
            interpret=INTERPRET,
        )(extended[:3], intact, weight, modulus_factor)
        padded_coupling = extended_2(coupling, (("gx", 0), ("gy", 1), ("gz", 2)), 3)
        displacement_now, velocity_now = pl.pallas_call(
            force_kernel,
            out_shape=(
                jax.ShapeDtypeStruct(displacement.shape, f32),
                jax.ShapeDtypeStruct(displacement.shape, f32),
            ),
            grid=(cells_x // ROWS,),
            in_specs=[
                whole((halo_x, cells_y + 6, cells_z + 6)),
                whole((halo_x, cells_y + 6, cells_z + 6)),
                bonds_spec,
                bonds_spec,
                vector_spec,
                vector_spec,
                vector_spec,
            ],
            out_specs=(vector_spec, vector_spec),
            scratch_shapes=[
                pltpu.VMEM((pairs, halo_x, cells_y, cells_z), f32),
                pltpu.VMEM((pairs, halo_x, cells_y, cells_z), f32),
            ],
            compiler_params=compiler_params(),
            interpret=INTERPRET,
        )(padded_coupling, padded_stiffness, stretches, intact, displacement_now, velocity_now, load_force)
    return (displacement_now, velocity_now)


def solution(mesh):
    placed = (
        P(None, "gx", "gy", "gz"),
        P(None, "gx", "gy", "gz"),
        P("gx", "gy", "gz"),
        P("gx", "gy", "gz"),
        P(None, "gx", "gy", "gz"),
        P("gx", "gy", "gz"),
        P(None, "gx", "gy", "gz"),
    )
    return jax.shard_map(
        local,
        mesh=mesh,
        in_specs=placed,
        out_specs=(P(None, "gx", "gy", "gz"), P(None, "gx", "gy", "gz")),
        check_vma=False,
    )
```

```python
import math

import jax
import jax.numpy as jnp
from jax import lax
from jax.experimental import pallas as pl
from jax.experimental.pallas import tpu as pltpu
from jax.sharding import PartitionSpec as P

STEPS = 2


TIME_STEP = 0.01

INTERPRET = False

ROWS = 4


def extended_2(cells, sides, width):
    for axis, dim in sides:
        count = lax.axis_size(axis)
        ends = count - 1
        head = lax.slice_in_dim(cells, 0, width, axis=dim)
        tail = lax.slice_in_dim(cells, cells.shape[dim] - width, cells.shape[dim], axis=dim)
        cells = jnp.concatenate(
            [
                lax.ppermute(tail.reshape(-1), axis, [(i, (i + 1) % count) for i in range(ends)]).reshape(tail.shape),
                cells,
                lax.ppermute(head.reshape(-1), axis, [((i + 1) % count, i) for i in range(ends)]).reshape(head.shape),
            ],
            axis=dim,
        )
    return cells


def offset_table():
    forward = []
    for step_x in range(-3, 4):
        for step_y in range(-3, 4):
            for step_z in range(-3, 4):
                squared = step_x * step_x + step_y * step_y + step_z * step_z
                if squared == 0 or squared > 9:
                    continue
                summed = step_x + step_y + step_z
                if summed > 0 or (summed == 0 and (step_x > 0 or (step_x == 0 and step_y > 0))):
                    forward.append((step_x, step_y, step_z))
    backward = []
    for entry in forward:
        backward.append((-entry[0], -entry[1], -entry[2]))
    return forward + backward


OFFSETS = offset_table()
LENGTHS = [math.sqrt(e[0] ** 2 + e[1] ** 2 + e[2] ** 2) for e in OFFSETS]
PAIRS = sorted({(e[1], e[2]) for e in OFFSETS} | {(0, 0)})
PAIR_OF = {pair: number for number, pair in enumerate(PAIRS)}


def presence(cell_count, device_index, device_count, offset_value):
    position = device_index * cell_count + jnp.arange(cell_count, dtype=jnp.int32) + offset_value
    return ((position >= 0) & (position < device_count * cell_count)).astype(jnp.float32)


def extend(values):
    return extended_2(values, (("gx", 1), ("gy", 2), ("gz", 3)), 3)


REACH = {pair: max(abs(e[0]) for e in OFFSETS if (e[1], e[2]) == pair) for pair in PAIRS if pair != (0, 0)}
REACH[(0, 0)] = 3


def fill_stack(stack_ref, padded_ref, leading):
    cells_y, cells_z = stack_ref.shape[-2], stack_ref.shape[-1]
    trips = 2
    chunk = stack_ref.shape[-3] // trips

    def rows(trip, carry):
        for pair, (oy, oz) in enumerate(PAIRS):
            skip = 3 - REACH[(oy, oz)]
            start = trip * chunk + skip * (1 - trip)
            count = chunk - skip
            for c in leading:
                target = (pair, pl.ds(start, count)) if c is None else (pair, c, pl.ds(start, count))
                source = (pl.ds(start, count),) if c is None else (c, pl.ds(start, count))
                stack_ref[target] = padded_ref[source + (pl.ds(3 + oy, cells_y), pl.ds(3 + oz, cells_z))]
        return carry

    lax.fori_loop(0, trips, rows, 0)


def stretch_kernel(ext_ref, intact_ref, weight_ref, factor_ref, stretch_ref, coupling_ref, us_ref):
    block = pl.program_id(0)

    @pl.when(block == 0)
    def _():
        fill_stack(us_ref, ext_ref, (0, 1, 2))

    centre = PAIR_OF[(0, 0)]
    x0 = pl.multiple_of(block * ROWS, ROWS)
    own = [us_ref[centre, c, pl.ds(x0 + 3, ROWS)] for c in range(3)]
    total = jnp.zeros_like(own[0])
    for number, entry in enumerate(OFFSETS):
        pair = PAIR_OF[(entry[1], entry[2])]
        squared = None
        for c in range(3):
            diff = us_ref[pair, c, pl.ds(x0 + 3 + entry[0], ROWS)] - own[c]
            if entry[c] != 0:
                diff = diff + float(entry[c])
            squared = diff * diff if squared is None else squared + diff * diff
        value = jnp.sqrt(squared) - LENGTHS[number]
        stretch_ref[number] = value
        total = total + intact_ref[number] * LENGTHS[number] * value
    weight = weight_ref[...]
    dilatation = 3.0 * total / weight
    coupling_ref[...] = dilatation * factor_ref[...] / weight


def force_kernel(pc_ref, ps_ref, stretch_ref, intact_ref, u_ref, v_ref, load_ref, unew_ref, vnew_ref, cs_ref, ss_ref):
    block = pl.program_id(0)

    @pl.when(block == 0)
    def _():
        fill_stack(cs_ref, pc_ref, (None,))
        fill_stack(ss_ref, ps_ref, (None,))

    centre = PAIR_OF[(0, 0)]
    x0 = pl.multiple_of(block * ROWS, ROWS)
    c_own = cs_ref[centre, pl.ds(x0 + 3, ROWS)]
    s_own = ss_ref[centre, pl.ds(x0 + 3, ROWS)]
    force = [None, None, None]
    for number, entry in enumerate(OFFSETS):
        pair = PAIR_OF[(entry[1], entry[2])]
        rows = pl.ds(x0 + 3 + entry[0], ROWS)
        scalar = intact_ref[number] * (
            LENGTHS[number] * (c_own + cs_ref[pair, rows])
            + (s_own + ss_ref[pair, rows]) * stretch_ref[number]
        )
        for c in range(3):
            if entry[c] != 0:
                term = scalar * (entry[c] / LENGTHS[number])
                force[c] = term if force[c] is None else force[c] + term
    for c in range(3):
        v_new = v_ref[c] + TIME_STEP * (force[c] + load_ref[c])
        vnew_ref[c] = v_new
        unew_ref[c] = u_ref[c] + TIME_STEP * v_new


def compiler_params():
    return pltpu.CompilerParams(vmem_limit_bytes=100 * 1024 * 1024)


def local(displacement, velocity, bulk_modulus, shear_modulus, blast_load, loaded, broken):
    count = len(OFFSETS)
    cell_shape = displacement.shape[1:]
    cells_x, cells_y, cells_z = cell_shape
    index_x = lax.axis_index("gx")
    index_y = lax.axis_index("gy")
    index_z = lax.axis_index("gz")
    span_x = lax.axis_size("gx")
    span_y = lax.axis_size("gy")
    span_z = lax.axis_size("gz")
    along_x = {value: presence(cells_x, index_x, span_x, value) for value in range(-3, 4)}
    along_y = {value: presence(cells_y, index_y, span_y, value) for value in range(-3, 4)}
    along_z = {value: presence(cells_z, index_z, span_z, value) for value in range(-3, 4)}
    exists_x = jnp.stack([along_x[e[0]] for e in OFFSETS])
    exists_y = jnp.stack([along_y[e[1]] for e in OFFSETS])
    exists_z = jnp.stack([along_z[e[2]] for e in OFFSETS])
    exists = exists_x[:, :, None, None] * exists_y[:, None, :, None] * exists_z[:, None, None, :]
    squares = jnp.array([l * l for l in LENGTHS], jnp.float32)
    weight = jnp.sum(exists * squares[:, None, None, None], axis=0)
    shifts = jnp.array([number % 8 for number in range(count)], jnp.int32)[:, None, None, None]
    words = jnp.repeat(broken, 8, axis=0)[:count]
    bits = jnp.right_shift(words, shifts) & 1
    intact = exists * (1.0 - bits.astype(jnp.float32))
    stiffness = 15.0 * shear_modulus / weight
    load_force = loaded.astype(jnp.float32)[None] * blast_load
    modulus_factor = 3.0 * bulk_modulus - 5.0 * shear_modulus
    displacement_now = displacement
    velocity_now = velocity
    padded_stiffness = None
    f32 = jnp.float32
    pairs = len(PAIRS)
    halo_x = cells_x + 6

    def whole(shape):
        return pl.BlockSpec(shape, lambda block: (0,) * len(shape))

    bonds_spec = pl.BlockSpec((count, ROWS, cells_y, cells_z), lambda block: (0, block, 0, 0))
    cells_spec = pl.BlockSpec((ROWS, cells_y, cells_z), lambda block: (block, 0, 0))
    vector_spec = pl.BlockSpec((3, ROWS, cells_y, cells_z), lambda block: (0, block, 0, 0))
    for step_index in range(STEPS):
        if step_index == 0:
            extended = extend(jnp.concatenate([displacement_now, stiffness[None]], axis=0))
            padded_stiffness = extended[3]
        else:
            extended = extend(displacement_now)
        stretches, coupling = pl.pallas_call(
            stretch_kernel,
            out_shape=(
                jax.ShapeDtypeStruct((count,) + tuple(cell_shape), f32),
                jax.ShapeDtypeStruct(tuple(cell_shape), f32),
            ),
            grid=(cells_x // ROWS,),
            in_specs=[
                whole((3, halo_x, cells_y + 6, cells_z + 6)),
                bonds_spec,
                cells_spec,
                cells_spec,
            ],
            out_specs=(bonds_spec, cells_spec),
            scratch_shapes=[pltpu.VMEM((pairs, 3, halo_x, cells_y, cells_z), f32)],
            compiler_params=compiler_params(),
            interpret=INTERPRET,
        )(extended[:3], intact, weight, modulus_factor)
        padded_coupling = extended_2(coupling, (("gx", 0), ("gy", 1), ("gz", 2)), 3)
        displacement_now, velocity_now = pl.pallas_call(
            force_kernel,
            out_shape=(
                jax.ShapeDtypeStruct(displacement.shape, f32),
                jax.ShapeDtypeStruct(displacement.shape, f32),
            ),
            grid=(cells_x // ROWS,),
            in_specs=[
                whole((halo_x, cells_y + 6, cells_z + 6)),
                whole((halo_x, cells_y + 6, cells_z + 6)),
                bonds_spec,
                bonds_spec,
                vector_spec,
                vector_spec,
                vector_spec,
            ],
            out_specs=(vector_spec, vector_spec),
            scratch_shapes=[
                pltpu.VMEM((pairs, halo_x, cells_y, cells_z), f32),
                pltpu.VMEM((pairs, halo_x, cells_y, cells_z), f32),
            ],
            compiler_params=compiler_params(),
            interpret=INTERPRET,
        )(padded_coupling, padded_stiffness, stretches, intact, displacement_now, velocity_now, load_force)
    return (displacement_now, velocity_now)


def solution(mesh):
    placed = (
        P(None, "gx", "gy", "gz"),
        P(None, "gx", "gy", "gz"),
        P("gx", "gy", "gz"),
        P("gx", "gy", "gz"),
        P(None, "gx", "gy", "gz"),
        P("gx", "gy", "gz"),
        P(None, "gx", "gy", "gz"),
    )
    return jax.shard_map(
        local,
        mesh=mesh,
        in_specs=placed,
        out_specs=(P(None, "gx", "gy", "gz"), P(None, "gx", "gy", "gz")),
        check_vma=False,
    )
```
